768 devices in a mesh: gx: 192 (over z, y, core), gy: 4 (over x).
Axes of the slice: x: 4, y: 8, z: 12, core: 2. Of those that a mesh axis runs over, the one named last changes fastest.
Arguments:
- moisture: float32 [49152, 20, 128], P(('gx', 'gy')), may hold values from 0.05 to 1
- diffusivity: float32 [49152, 20, 128], P(('gx', 'gy')), may hold values from 0.1 to 4
- rain: float32 [49152, 128], P(('gx', 'gy')), may hold values from 0 to 2
- head: float32 [50, 3072, 512], P(None, 'gx', 'gy'), may hold values from -4 to 4
- conductivity: float32 [50, 3072, 512], P(None, 'gx', 'gy'), may hold values from 0.05 to 1
- tile_ids: int32 [49152], P(('gx', 'gy')), may hold values from 0 to 3, as said below
- offsets: int32 [49152], P(('gx', 'gy')), may hold values from 0 to 15
- patch_ids: int32 [49152], P(('gx', 'gy')), may hold values from 0 to 7
- counts: int32 [768], P(('gx', 'gy')), may hold values from 48 to 64, as said below
Outputs:
- head_out: float32 [50, 3072, 512], P(None, 'gx', 'gy')
- moisture_out: float32 [49152, 20, 128], P(('gx', 'gy'))
- patch_sums: float32 [6144, 128], P(('gx', 'gy'))
The draws below stay inside these ranges and needn't reach their ends.
Inputs may be any that keep to these rules, and one draw needn't show every extreme that they name: `tile_ids`: only the first counts[d] block slots of device d are used; the others' entries are arbitrary. Among the used blocks of one device at most 32 name the same tile, and in every gx row one tile is named by exactly 32 used blocks of every device of that row. `counts`: some device uses all 64 slots in every draw.
All inputs are finite; a program needn't handle non-finite values.
Results may differ from the reference program's by a relative error of at most 0.00016.
Values sent between devices are 32-bit elements; how exact they have to be, the bound alone decides.
No kernel may reach another device: no remote copies, remote signals or barrier semaphores. Data moves between devices by JAX's collectives and lax.ppermute only.
A program may use at most 32 MiB of HBM per device.

```python
import math
import jax
import jax.numpy as jnp
from jax import lax

NZ = 50
LAYERS = 20
COLS = 128
CX = 16
LB = 64
PATCH_DEV = 8
SWEEPS = 6
NX = 3072
NY = 512
BLOCKS = 49152
PATCHES = 6144
N_GX = 192
N_GY = 4


def block_layout(key):
    device_count = N_GX * N_GY
    half = LB // 2
    base_key = jax.random.fold_in(key, 11)
    key_count, key_star, key_other, key_order, key_rows, key_patch = jax.random.split(base_key, 6)
    used_counts = jax.random.randint(key_count, (device_count,), (half + LB) // 2, LB + 1)
    used_counts = jnp.where(jnp.arange(device_count) == 0, LB, used_counts).astype(jnp.int32)
    star_row = jax.random.randint(key_star, (N_GX,), 0, N_GY)
    star_dev = jnp.repeat(star_row, N_GY)
    stride = jax.random.randint(key_other, (device_count, LB), 1, N_GY)
    position = jnp.arange(LB, dtype=jnp.int32)
    ordered = jnp.where(position[None, :] < half, star_dev[:, None], (star_dev[:, None] + stride) % N_GY)
    scores = jax.random.randint(key_order, (device_count, LB), 0, 2 ** 20) * LB + position[None, :]
    scores = jnp.where(position[None, :] < used_counts[:, None], scores, 2 ** 28 + position[None, :])
    shuffle = jnp.argsort(scores, axis=1)
    tiles = jnp.take_along_axis(ordered, shuffle, axis=1).reshape(-1).astype(jnp.int32)
    grid_rows = jax.random.randint(key_rows, (device_count * LB,), 0, CX).astype(jnp.int32)
    patches = jax.random.randint(key_patch, (device_count * LB,), 0, PATCH_DEV).astype(jnp.int32)
    return (tiles, grid_rows, patches, used_counts)


def draw_tile_ids(key, part):
    return block_layout(key)[0]


def draw_offsets(key, part):
    return block_layout(key)[1]


def draw_patch_ids(key, part):
    return block_layout(key)[2]


def draw_counts(key, part):
    return block_layout(key)[3]


def draw_head(key, part):
    return jax.random.truncated_normal(key, -4.0, 4.0, (NZ, NX, NY), jnp.float32)


def block_scale(key, shape, shards, smallest, high):
    level, own = 1.0, jax.random.fold_in(key, 6)
    for dim, blocks in shards:
        heights = jnp.exp(jax.random.uniform(jax.random.fold_in(own, dim), (blocks,), jnp.float32, smallest / len(shards), high / len(shards)))
        level = level * jnp.repeat(heights, shape[dim] // blocks).reshape([-1 if axis == dim else 1 for axis in range(len(shape))])
    return level


def setup_inputs(seed: int = 0) -> dict:
    seeds = jax.random.split(jax.random.key(seed), 10)
    return {
        "moisture": jnp.clip(jnp.exp(math.log(1.0) - 2.9957323 * jax.random.uniform(seeds[0], (BLOCKS, LAYERS, COLS), jnp.float32) ** block_scale(seeds[0], (BLOCKS, LAYERS, COLS), ((0, 768),), -0.2, 0.2)), 0.05, 1.0),
        "diffusivity": jnp.clip(jnp.exp(math.log(4.0) - 3.6888794 * jax.random.uniform(seeds[1], (BLOCKS, LAYERS, COLS), jnp.float32) ** block_scale(seeds[1], (BLOCKS, LAYERS, COLS), ((0, 768),), -0.2, 0.2)), 0.1, 4.0),
        "rain": jnp.clip(2.0 * jax.random.uniform(seeds[2], (BLOCKS, COLS), jnp.float32) ** block_scale(seeds[2], (BLOCKS, COLS), ((0, 768),), -0.2, 0.2), 0.0, 2.0),
        "head": draw_head(jax.random.fold_in(seeds[9], 71), 0),
        "conductivity": jnp.clip(jnp.exp(math.log(1.0) - 2.9957323 * jax.random.uniform(seeds[4], (NZ, NX, NY), jnp.float32) ** block_scale(seeds[4], (NZ, NX, NY), ((1, 192), (2, 4)), -0.2, 0.2)), 0.05, 1.0),
        "tile_ids": draw_tile_ids(jax.random.fold_in(seeds[9], 71), 0),
        "offsets": draw_offsets(jax.random.fold_in(seeds[9], 71), 0),
        "patch_ids": draw_patch_ids(jax.random.fold_in(seeds[9], 71), 0),
        "counts": draw_counts(jax.random.fold_in(seeds[9], 71), 0),
    }


flow_rate = 0.15
capillary = 0.5


def column_solve(moisture, diffusivity, rain):
    depth = moisture.shape[1]
    ratios = []
    forward_vals = []
    for layer_k in range(depth):
        lower_coef = diffusivity[:, layer_k, :]
        source = moisture[:, layer_k, :]
        if layer_k == 0:
            source = source + rain
            pivot = 1.0 + lower_coef
            carried = source / pivot
        else:
            upper_coef = diffusivity[:, layer_k - 1, :]
            pivot = 1.0 + lower_coef + upper_coef - upper_coef * ratios[-1]
            carried = (source + upper_coef * forward_vals[-1]) / pivot
        ratios.append(lower_coef / pivot)
        forward_vals.append(carried)
    solved = [forward_vals[-1]]
    for layer_k in range(depth - 2, -1, -1):
        solved.append(forward_vals[layer_k] + ratios[layer_k] * solved[-1])
    return jnp.stack(solved[::-1], axis=1)


def lateral_core(padded_head, padded_cond):
    inner_rows = padded_head.shape[1] - 2
    inner_cols = padded_head.shape[2] - 2
    centre = padded_head[:, 1:-1, 1:-1]
    centre_cond = padded_cond[:, 1:-1, 1:-1]
    flux_total = jnp.zeros_like(centre)
    for row_shift, col_shift in ((0, 1), (2, 1), (1, 0), (1, 2)):
        beside = padded_head[:, row_shift:row_shift + inner_rows, col_shift:col_shift + inner_cols]
        beside_cond = padded_cond[:, row_shift:row_shift + inner_rows, col_shift:col_shift + inner_cols]
        flux_total = flux_total + 0.5 * (centre_cond + beside_cond) * (beside - centre)
    vertical = 0.5 * (centre_cond[1:] + centre_cond[:-1]) * (centre[1:] - centre[:-1])
    flux_total = flux_total + jnp.pad(vertical, ((0, 1), (0, 0), (0, 0))) - jnp.pad(vertical, ((1, 0), (0, 0), (0, 0)))
    return centre + flow_rate * flux_total


def solve_group(grouped):
    return column_solve(grouped[0], grouped[1], grouped[2])


def reference(moisture, diffusivity, rain, head, conductivity, tile_ids, offsets, patch_ids, counts):
    device_count = N_GX * N_GY
    wet = lax.map(solve_group, (moisture.reshape(device_count, LB, LAYERS, COLS),
                                diffusivity.reshape(device_count, LB, LAYERS, COLS),
                                rain.reshape(device_count, LB, COLS)))
    wet = wet.reshape(BLOCKS, LAYERS, COLS)
    bottom = wet[:, LAYERS - 1, :]
    drain = diffusivity[:, LAYERS - 1, :] * bottom
    block_index = jnp.arange(BLOCKS, dtype=jnp.int32)
    owner = block_index // LB
    in_use = (block_index % LB) < counts[owner]
    in_use_f = in_use.astype(jnp.float32)
    grid_rows = (owner // N_GY) * CX + offsets
    grid_cols = tile_ids[:, None] * COLS + jnp.arange(COLS, dtype=jnp.int32)[None, :]
    surface = head[0].at[grid_rows[:, None], grid_cols].add(drain * in_use_f[:, None])
    field = head.at[0].set(surface)
    padding = ((0, 0), (1, 1), (1, 1))
    padded_cond = jnp.pad(conductivity, padding)
    for sweep_k in range(SWEEPS):
        field = lateral_core(jnp.pad(field, padding), padded_cond)
    saturation = field[0][grid_rows[:, None], grid_cols] * in_use_f[:, None]
    new_bottom = bottom + capillary * (saturation - in_use_f[:, None] * bottom)
    moisture_out = wet.at[:, LAYERS - 1, :].set(new_bottom)
    patch_global = owner * PATCH_DEV + patch_ids
    patch_sums = jax.ops.segment_sum(saturation, patch_global, num_segments=PATCHES)
    return (field, moisture_out, patch_sums)
```

```python
import jax
import jax.numpy as jnp
from jax import lax
from jax.sharding import PartitionSpec as P

PATCH_DEV = 8
SWEEPS = 6


flow_rate = 0.15
capillary = 0.5


def with_halo(cells, sides, width):
    for axis, dim in sides:
        count = lax.axis_size(axis)
        ends = count - 1
        head = lax.slice_in_dim(cells, 0, width, axis=dim)
        tail = lax.slice_in_dim(cells, cells.shape[dim] - width, cells.shape[dim], axis=dim)
        cells = jnp.concatenate(
            [
                lax.ppermute(tail, axis, [(i, (i + 1) % count) for i in range(ends)]),
                cells,
                lax.ppermute(head, axis, [((i + 1) % count, i) for i in range(ends)]),
            ],
            axis=dim,
        )
    return cells


def column_solve(moisture, diffusivity, rain):
    depth = moisture.shape[1]
    ratios = []
    forward_vals = []
    for layer_k in range(depth):
        lower_coef = diffusivity[:, layer_k, :]
        source = moisture[:, layer_k, :]
        if layer_k == 0:
            source = source + rain
            pivot = 1.0 + lower_coef
            carried = source / pivot
        else:
            upper_coef = diffusivity[:, layer_k - 1, :]
            pivot = 1.0 + lower_coef + upper_coef - upper_coef * ratios[-1]
            carried = (source + upper_coef * forward_vals[-1]) / pivot
        ratios.append(lower_coef / pivot)
        forward_vals.append(carried)
    solved = [forward_vals[-1]]
    for layer_k in range(depth - 2, -1, -1):
        solved.append(forward_vals[layer_k] + ratios[layer_k] * solved[-1])
    return jnp.stack(solved[::-1], axis=1)


def lateral_core(padded_head, padded_cond):
    inner_rows = padded_head.shape[1] - 2
    inner_cols = padded_head.shape[2] - 2
    centre = padded_head[:, 1:-1, 1:-1]
    centre_cond = padded_cond[:, 1:-1, 1:-1]
    flux_total = jnp.zeros_like(centre)
    for row_shift, col_shift in ((0, 1), (2, 1), (1, 0), (1, 2)):
        beside = padded_head[
            :, row_shift : row_shift + inner_rows, col_shift : col_shift + inner_cols
        ]
        beside_cond = padded_cond[
            :, row_shift : row_shift + inner_rows, col_shift : col_shift + inner_cols
        ]
        flux_total = flux_total + 0.5 * (centre_cond + beside_cond) * (beside - centre)
    vertical = 0.5 * (centre_cond[1:] + centre_cond[:-1]) * (centre[1:] - centre[:-1])
    flux_total = (
        flux_total
        + jnp.pad(vertical, ((0, 1), (0, 0), (0, 0)))
        - jnp.pad(vertical, ((1, 0), (0, 0), (0, 0)))
    )
    return centre + flow_rate * flux_total


def local(moisture, diffusivity, rain, head, conductivity, tile_ids, offsets, patch_ids, counts):
    highest = lax.Precision.HIGHEST
    block_count = moisture.shape[0]
    tile_count = lax.axis_size("gy")
    capacity = block_count // 2
    tile_rows = head.shape[1]
    tile_cols = head.shape[2]
    wet = column_solve(moisture, diffusivity, rain)
    bottom = wet[:, -1, :]
    drain = diffusivity[:, -1, :] * bottom
    in_use = jnp.arange(block_count, dtype=jnp.int32) < counts[0]
    in_use_f = in_use.astype(jnp.float32)
    to_tile = (
        (tile_ids[:, None] == jnp.arange(tile_count, dtype=jnp.int32)[None, :]) & in_use[:, None]
    ).astype(jnp.int32)
    before = jnp.cumsum(to_tile, axis=0) - to_tile
    slot_of = jnp.sum(before * to_tile, axis=1)
    slot_match = slot_of[None, None, :] == jnp.arange(capacity, dtype=jnp.int32)[None, :, None]
    placing = (to_tile.T[:, None, :] * slot_match).astype(jnp.float32)
    outgoing = jnp.einsum("tcb,bj->tcj", placing, drain, precision=highest)
    out_rows = (
        jnp.einsum("tcb,b->tc", placing, (offsets + 1).astype(jnp.float32), precision=highest) - 1.0
    )
    packed = jnp.concatenate(
        [outgoing, jnp.pad(out_rows, ((0, 0), (0, tile_cols - capacity)))[:, None, :]], axis=1
    )
    arrived = lax.all_to_all(packed, "gy", split_axis=0, concat_axis=0, tiled=True)
    incoming = arrived[:, :capacity, :]
    in_rows = arrived[:, capacity, :capacity]
    slot_total = tile_count * capacity
    landing = (
        in_rows.reshape(1, slot_total) == jnp.arange(tile_rows, dtype=jnp.float32)[:, None]
    ).astype(jnp.float32)
    recharge = jnp.dot(landing, incoming.reshape(slot_total, tile_cols), precision=highest)
    field = head.at[0].add(recharge)
    layers = field.shape[0]
    both = with_halo(
        jnp.concatenate([field, conductivity], axis=0), (("gx", 1), ("gy", 2)), SWEEPS
    )
    field = both[:layers]
    padded_cond = both[layers:]
    row_at = (
        lax.axis_index("gx") * tile_rows - SWEEPS + jnp.arange(tile_rows + 2 * SWEEPS)
    )[:, None]
    col_at = (
        lax.axis_index("gy") * tile_cols - SWEEPS + jnp.arange(tile_cols + 2 * SWEEPS)
    )[None, :]
    inside = (
        (row_at >= 0)
        & (row_at < tile_rows * lax.axis_size("gx"))
        & (col_at >= 0)
        & (col_at < tile_cols * tile_count)
    )
    for sweep_k in range(SWEEPS):
        field = lateral_core(field, padded_cond)
        padded_cond = padded_cond[:, 1:-1, 1:-1]
        if sweep_k < SWEEPS - 1:
            edge = sweep_k + 1
            field = jnp.where(inside[None, edge:-edge, edge:-edge], field, 0.0)
    surface = field[0]
    answered = jnp.dot(landing.T, surface, precision=highest).reshape(
        tile_count, capacity, tile_cols
    )
    returned = lax.all_to_all(answered, "gy", split_axis=0, concat_axis=0, tiled=True)
    saturation = jnp.einsum("tcb,tcj->bj", placing, returned, precision=highest)
    new_bottom = bottom + capillary * (saturation - in_use_f[:, None] * bottom)
    moisture_out = wet.at[:, -1, :].set(new_bottom)
    patch_hot = (patch_ids[None, :] == jnp.arange(PATCH_DEV, dtype=jnp.int32)[:, None]).astype(
        jnp.float32
    )
    patch_sums = jnp.dot(patch_hot, saturation, precision=highest)
    return (field, moisture_out, patch_sums)


def solution(mesh):
    placed = (
        P(("gx", "gy"), None, None),
        P(("gx", "gy"), None, None),
        P(("gx", "gy"), None),
        P(None, "gx", "gy"),
        P(None, "gx", "gy"),
        P(("gx", "gy")),
        P(("gx", "gy")),
        P(("gx", "gy")),
        P(("gx", "gy")),
    )
    return jax.shard_map(
        local,
        mesh=mesh,
        in_specs=placed,
        out_specs=(P(None, "gx", "gy"), P(("gx", "gy"), None, None), P(("gx", "gy"), None)),
        check_vma=False,
    )
```

```python
import jax
import jax.numpy as jnp
from jax import lax
from jax.sharding import PartitionSpec as P

PATCH_DEV = 8
SWEEPS = 6


flow_rate = 0.15
capillary = 0.5


def with_halo(cells, sides, width):
    for axis, dim in sides:
        count = lax.axis_size(axis)
        ends = count - 1
        head = lax.slice_in_dim(cells, 0, width, axis=dim)
        tail = lax.slice_in_dim(cells, cells.shape[dim] - width, cells.shape[dim], axis=dim)
        cells = jnp.concatenate(
            [
                lax.ppermute(tail, axis, [(i, (i + 1) % count) for i in range(ends)]),
                cells,
                lax.ppermute(head, axis, [((i + 1) % count, i) for i in range(ends)]),
            ],
            axis=dim,
        )
    return cells


def column_solve(moisture, diffusivity, rain):
    depth = moisture.shape[1]
    ratios = []
    forward_vals = []
    for layer_k in range(depth):
        lower_coef = diffusivity[:, layer_k, :]
        source = moisture[:, layer_k, :]
        if layer_k == 0:
            source = source + rain
            pivot = 1.0 + lower_coef
            carried = source / pivot
        else:
            upper_coef = diffusivity[:, layer_k - 1, :]
            pivot = 1.0 + lower_coef + upper_coef - upper_coef * ratios[-1]
            carried = (source + upper_coef * forward_vals[-1]) / pivot
        ratios.append(lower_coef / pivot)
        forward_vals.append(carried)
    solved = [forward_vals[-1]]
    for layer_k in range(depth - 2, -1, -1):
        solved.append(forward_vals[layer_k] + ratios[layer_k] * solved[-1])
    return solved[::-1]


def lateral_core(padded_head, padded_cond):
    inner_rows = padded_head.shape[1] - 2
    inner_cols = padded_head.shape[2] - 2
    centre = padded_head[:, 1:-1, 1:-1]
    centre_cond = padded_cond[:, 1:-1, 1:-1]
    flux_total = jnp.zeros_like(centre)
    for row_shift, col_shift in ((0, 1), (2, 1), (1, 0), (1, 2)):
        beside = padded_head[
            :, row_shift : row_shift + inner_rows, col_shift : col_shift + inner_cols
        ]
        beside_cond = padded_cond[
            :, row_shift : row_shift + inner_rows, col_shift : col_shift + inner_cols
        ]
        flux_total = flux_total + 0.5 * (centre_cond + beside_cond) * (beside - centre)
    vertical = 0.5 * (centre_cond[1:] + centre_cond[:-1]) * (centre[1:] - centre[:-1])
    flux_total = (
        flux_total
        + jnp.pad(vertical, ((0, 1), (0, 0), (0, 0)))
        - jnp.pad(vertical, ((1, 0), (0, 0), (0, 0)))
    )
    return centre + flow_rate * flux_total


def local(moisture, diffusivity, rain, head, conductivity, tile_ids, offsets, patch_ids, counts):
    highest = lax.Precision.HIGHEST
    block_count = moisture.shape[0]
    tile_count = lax.axis_size("gy")
    capacity = block_count // 2
    tile_rows = head.shape[1]
    tile_cols = head.shape[2]
    wet = column_solve(moisture, diffusivity, rain)
    bottom = wet[-1]
    drain = diffusivity[:, -1, :] * bottom
    in_use = jnp.arange(block_count, dtype=jnp.int32) < counts[0]
    in_use_f = in_use.astype(jnp.float32)
    to_tile = (
        (tile_ids[:, None] == jnp.arange(tile_count, dtype=jnp.int32)[None, :]) & in_use[:, None]
    ).astype(jnp.int32)
    before = jnp.cumsum(to_tile, axis=0) - to_tile
    slot_of = jnp.sum(before * to_tile, axis=1)
    slot_match = slot_of[None, None, :] == jnp.arange(capacity, dtype=jnp.int32)[None, :, None]
    placing = (to_tile.T[:, None, :] * slot_match).astype(jnp.float32)
    outgoing = jnp.einsum("tcb,bj->tcj", placing, drain, precision=highest)
    out_rows = (
        jnp.einsum("tcb,b->tc", placing, (offsets + 1).astype(jnp.float32), precision=highest) - 1.0
    )
    packed = jnp.concatenate(
        [outgoing, jnp.pad(out_rows, ((0, 0), (0, tile_cols - capacity)))[:, None, :]], axis=1
    )
    arrived = lax.all_to_all(packed, "gy", split_axis=0, concat_axis=0, tiled=True)
    incoming = arrived[:, :capacity, :]
    in_rows = arrived[:, capacity, :capacity]
    slot_total = tile_count * capacity
    landing = (
        in_rows.reshape(1, slot_total) == jnp.arange(tile_rows, dtype=jnp.float32)[:, None]
    ).astype(jnp.float32)
    recharge = jnp.dot(landing, incoming.reshape(slot_total, tile_cols), precision=highest)
    layers = head.shape[0]
    sides = (("gx", 1), ("gy", 2))
    rest = with_halo(jnp.concatenate([head[1:], conductivity], axis=0), sides, SWEEPS)
    top = with_halo(head[:1] + recharge[None], sides, SWEEPS)
    field = jnp.concatenate([top, rest[: layers - 1]], axis=0)
    padded_cond = rest[layers - 1 :]
    row_at = (
        lax.axis_index("gx") * tile_rows - SWEEPS + jnp.arange(tile_rows + 2 * SWEEPS)
    )[:, None]
    col_at = (
        lax.axis_index("gy") * tile_cols - SWEEPS + jnp.arange(tile_cols + 2 * SWEEPS)
    )[None, :]
    inside = (
        (row_at >= 0)
        & (row_at < tile_rows * lax.axis_size("gx"))
        & (col_at >= 0)
        & (col_at < tile_cols * tile_count)
    )
    for sweep_k in range(SWEEPS):
        field = lateral_core(field, padded_cond)
        padded_cond = padded_cond[:, 1:-1, 1:-1]
        if sweep_k < SWEEPS - 1:
            edge = sweep_k + 1
            field = jnp.where(inside[None, edge:-edge, edge:-edge], field, 0.0)
    surface = field[0]
    answered = jnp.dot(landing.T, surface, precision=highest).reshape(
        tile_count, capacity, tile_cols
    )
    returned = lax.all_to_all(answered, "gy", split_axis=0, concat_axis=0, tiled=True)
    saturation = jnp.einsum("tcb,tcj->bj", placing, returned, precision=highest)
    new_bottom = bottom + capillary * (saturation - in_use_f[:, None] * bottom)
    moisture_out = jnp.stack(wet[:-1] + [new_bottom], axis=1)
    patch_hot = (patch_ids[None, :] == jnp.arange(PATCH_DEV, dtype=jnp.int32)[:, None]).astype(
        jnp.float32
    )
    patch_sums = jnp.dot(patch_hot, saturation, precision=highest)
    return (field, moisture_out, patch_sums)


def solution(mesh):
    placed = (
        P(("gx", "gy"), None, None),
        P(("gx", "gy"), None, None),
        P(("gx", "gy"), None),
        P(None, "gx", "gy"),
        P(None, "gx", "gy"),
        P(("gx", "gy")),
        P(("gx", "gy")),
        P(("gx", "gy")),
        P(("gx", "gy")),
    )
    return jax.shard_map(
        local,
        mesh=mesh,
        in_specs=placed,
        out_specs=(P(None, "gx", "gy"), P(("gx", "gy"), None, None), P(("gx", "gy"), None)),
        check_vma=False,
    )
```

```python
import jax
import jax.numpy as jnp
from jax import lax
from jax.sharding import PartitionSpec as P
from jax.experimental import pallas as pl
from jax.experimental.pallas import tpu as pltpu

PATCH_DEV = 8
SWEEPS = 6


flow_rate = 0.15
capillary = 0.5


def with_halo(cells, sides, width):
    for axis, dim in sides:
        count = lax.axis_size(axis)
        ends = count - 1
        head = lax.slice_in_dim(cells, 0, width, axis=dim)
        tail = lax.slice_in_dim(cells, cells.shape[dim] - width, cells.shape[dim], axis=dim)
        cells = jnp.concatenate(
            [
                lax.ppermute(tail, axis, [(i, (i + 1) % count) for i in range(ends)]),
                cells,
                lax.ppermute(head, axis, [((i + 1) % count, i) for i in range(ends)]),
            ],
            axis=dim,
        )
    return cells


def column_kernel(moist_ref, diff_ref, rain_ref, wet_ref, ratio_ref):
    lanes = rain_ref.shape[1]
    depth = moist_ref.shape[1] // lanes
    group = 8

    def layer(ref, rows, k):
        return ref[rows, k * lanes : (k + 1) * lanes]

    def body(g, carry):
        rows = pl.ds(pl.multiple_of(g * group, group), group)
        ratio = None
        carried = None
        for layer_k in range(depth):
            lower_coef = layer(diff_ref, rows, layer_k)
            source = layer(moist_ref, rows, layer_k)
            if layer_k == 0:
                source = source + rain_ref[rows, :]
                pivot = 1.0 + lower_coef
                carried = source / pivot
            else:
                upper_coef = layer(diff_ref, rows, layer_k - 1)
                pivot = 1.0 + lower_coef + upper_coef - upper_coef * ratio
                carried = (source + upper_coef * carried) / pivot
            ratio = lower_coef / pivot
            ratio_ref[rows, layer_k * lanes : (layer_k + 1) * lanes] = ratio
            wet_ref[rows, layer_k * lanes : (layer_k + 1) * lanes] = carried
        solved = carried
        for layer_k in range(depth - 2, -1, -1):
            solved = layer(wet_ref, rows, layer_k) + layer(ratio_ref, rows, layer_k) * solved
            wet_ref[rows, layer_k * lanes : (layer_k + 1) * lanes] = solved
        return carry

    lax.fori_loop(0, moist_ref.shape[0] // group, body, 0)


def column_solve(moisture, diffusivity, rain):
    blocks, depth, lanes = moisture.shape
    flat = (blocks, depth * lanes)
    wet = pl.pallas_call(
        column_kernel,
        out_shape=jax.ShapeDtypeStruct(flat, jnp.float32),
        in_specs=[pl.BlockSpec(memory_space=pltpu.VMEM)] * 3,
        out_specs=pl.BlockSpec(memory_space=pltpu.VMEM),
        scratch_shapes=[pltpu.VMEM(flat, jnp.float32)],
        cost_estimate=pl.CostEstimate(
            flops=12 * blocks * depth * lanes, transcendentals=0, bytes_accessed=12 * blocks * depth * lanes
        ),
    )(moisture.reshape(flat), diffusivity.reshape(flat), rain)
    return wet


def lateral_core(padded_head, padded_cond):
    inner_rows = padded_head.shape[1] - 2
    inner_cols = padded_head.shape[2] - 2
    centre = padded_head[:, 1:-1, 1:-1]
    centre_cond = padded_cond[:, 1:-1, 1:-1]
    flux_total = jnp.zeros_like(centre)
    for row_shift, col_shift in ((0, 1), (2, 1), (1, 0), (1, 2)):
        beside = padded_head[
            :, row_shift : row_shift + inner_rows, col_shift : col_shift + inner_cols
        ]
        beside_cond = padded_cond[
            :, row_shift : row_shift + inner_rows, col_shift : col_shift + inner_cols
        ]
        flux_total = flux_total + 0.5 * (centre_cond + beside_cond) * (beside - centre)
    vertical = 0.5 * (centre_cond[1:] + centre_cond[:-1]) * (centre[1:] - centre[:-1])
    flux_total = (
        flux_total
        + jnp.pad(vertical, ((0, 1), (0, 0), (0, 0)))
        - jnp.pad(vertical, ((1, 0), (0, 0), (0, 0)))
    )
    return centre + flow_rate * flux_total


def local(moisture, diffusivity, rain, head, conductivity, tile_ids, offsets, patch_ids, counts):
    highest = lax.Precision.HIGHEST
    block_count = moisture.shape[0]
    tile_count = lax.axis_size("gy")
    capacity = block_count // 2
    tile_rows = head.shape[1]
    tile_cols = head.shape[2]
    wet = column_solve(moisture, diffusivity, rain)
    depth = moisture.shape[1]
    bottom = wet[:, (depth - 1) * tile_cols :]
    drain = diffusivity[:, -1, :] * bottom
    in_use = jnp.arange(block_count, dtype=jnp.int32) < counts[0]
    in_use_f = in_use.astype(jnp.float32)
    to_tile = (
        (tile_ids[:, None] == jnp.arange(tile_count, dtype=jnp.int32)[None, :]) & in_use[:, None]
    ).astype(jnp.int32)
    before = jnp.cumsum(to_tile, axis=0) - to_tile
    slot_of = jnp.sum(before * to_tile, axis=1)
    slot_match = slot_of[None, None, :] == jnp.arange(capacity, dtype=jnp.int32)[None, :, None]
    placing = (to_tile.T[:, None, :] * slot_match).astype(jnp.float32)
    outgoing = jnp.einsum("tcb,bj->tcj", placing, drain, precision=highest)
    out_rows = (
        jnp.einsum("tcb,b->tc", placing, (offsets + 1).astype(jnp.float32), precision=highest) - 1.0
    )
    packed = jnp.concatenate(
        [outgoing, jnp.pad(out_rows, ((0, 0), (0, tile_cols - capacity)))[:, None, :]], axis=1
    )
    arrived = lax.all_to_all(packed, "gy", split_axis=0, concat_axis=0, tiled=True)
    incoming = arrived[:, :capacity, :]
    in_rows = arrived[:, capacity, :capacity]
    slot_total = tile_count * capacity
    landing = (
        in_rows.reshape(1, slot_total) == jnp.arange(tile_rows, dtype=jnp.float32)[:, None]
    ).astype(jnp.float32)
    recharge = jnp.dot(landing, incoming.reshape(slot_total, tile_cols), precision=highest)
    field = head.at[0].add(recharge)
    layers = field.shape[0]
    both = with_halo(
        jnp.concatenate([field, conductivity], axis=0), (("gx", 1), ("gy", 2)), SWEEPS
    )
    field = both[:layers]
    padded_cond = both[layers:]
    row_at = (
        lax.axis_index("gx") * tile_rows - SWEEPS + jnp.arange(tile_rows + 2 * SWEEPS)
    )[:, None]
    col_at = (
        lax.axis_index("gy") * tile_cols - SWEEPS + jnp.arange(tile_cols + 2 * SWEEPS)
    )[None, :]
    inside = (
        (row_at >= 0)
        & (row_at < tile_rows * lax.axis_size("gx"))
        & (col_at >= 0)
        & (col_at < tile_cols * tile_count)
    )
    for sweep_k in range(SWEEPS):
        field = lateral_core(field, padded_cond)
        padded_cond = padded_cond[:, 1:-1, 1:-1]
        if sweep_k < SWEEPS - 1:
            edge = sweep_k + 1
            field = jnp.where(inside[None, edge:-edge, edge:-edge], field, 0.0)
    surface = field[0]
    answered = jnp.dot(landing.T, surface, precision=highest).reshape(
        tile_count, capacity, tile_cols
    )
    returned = lax.all_to_all(answered, "gy", split_axis=0, concat_axis=0, tiled=True)
    saturation = jnp.einsum("tcb,tcj->bj", placing, returned, precision=highest)
    new_bottom = bottom + capillary * (saturation - in_use_f[:, None] * bottom)
    moisture_out = jnp.concatenate(
        [wet[:, : (depth - 1) * tile_cols], new_bottom], axis=1
    ).reshape(moisture.shape)
    patch_hot = (patch_ids[None, :] == jnp.arange(PATCH_DEV, dtype=jnp.int32)[:, None]).astype(
        jnp.float32
    )
    patch_sums = jnp.dot(patch_hot, saturation, precision=highest)
    return (field, moisture_out, patch_sums)


def solution(mesh):
    placed = (
        P(("gx", "gy"), None, None),
        P(("gx", "gy"), None, None),
        P(("gx", "gy"), None),
        P(None, "gx", "gy"),
        P(None, "gx", "gy"),
        P(("gx", "gy")),
        P(("gx", "gy")),
        P(("gx", "gy")),
        P(("gx", "gy")),
    )
    return jax.shard_map(
        local,
        mesh=mesh,
        in_specs=placed,
        out_specs=(P(None, "gx", "gy"), P(("gx", "gy"), None, None), P(("gx", "gy"), None)),
        check_vma=False,
    )
```

```python
import jax
import jax.numpy as jnp
from jax import lax
from jax.sharding import PartitionSpec as P
from jax.experimental import pallas as pl
from jax.experimental.pallas import tpu as pltpu

PATCH_DEV = 8
SWEEPS = 6


flow_rate = 0.15
capillary = 0.5


def with_halo(cells, sides, width):
    for axis, dim in sides:
        count = lax.axis_size(axis)
        ends = count - 1
        head = lax.slice_in_dim(cells, 0, width, axis=dim)
        tail = lax.slice_in_dim(cells, cells.shape[dim] - width, cells.shape[dim], axis=dim)
        cells = jnp.concatenate(
            [
                lax.ppermute(tail, axis, [(i, (i + 1) % count) for i in range(ends)]),
                cells,
                lax.ppermute(head, axis, [((i + 1) % count, i) for i in range(ends)]),
            ],
            axis=dim,
        )
    return cells


def column_kernel(moist_ref, diff_ref, rain_ref, wet_ref, ratio_ref):
    lanes = rain_ref.shape[1]
    depth = moist_ref.shape[1] // lanes
    group = 8

    def layer(ref, rows, k):
        return ref[rows, k * lanes : (k + 1) * lanes]

    def body(g, carry):
        rows = pl.ds(pl.multiple_of(g * group, group), group)
        ratio = None
        carried = None
        for layer_k in range(depth):
            lower_coef = layer(diff_ref, rows, layer_k)
            source = layer(moist_ref, rows, layer_k)
            if layer_k == 0:
                source = source + rain_ref[rows, :]
                pivot = 1.0 + lower_coef
                carried = source / pivot
            else:
                upper_coef = layer(diff_ref, rows, layer_k - 1)
                pivot = 1.0 + lower_coef + upper_coef - upper_coef * ratio
                carried = (source + upper_coef * carried) / pivot
            ratio = lower_coef / pivot
            ratio_ref[rows, layer_k * lanes : (layer_k + 1) * lanes] = ratio
            wet_ref[rows, layer_k * lanes : (layer_k + 1) * lanes] = carried
        solved = carried
        for layer_k in range(depth - 2, -1, -1):
            solved = layer(wet_ref, rows, layer_k) + layer(ratio_ref, rows, layer_k) * solved
            wet_ref[rows, layer_k * lanes : (layer_k + 1) * lanes] = solved
        return carry

    lax.fori_loop(0, moist_ref.shape[0] // group, body, 0)


def column_solve(moisture, diffusivity, rain):
    blocks, depth, lanes = moisture.shape
    flat = (blocks, depth * lanes)
    wet = pl.pallas_call(
        column_kernel,
        out_shape=jax.ShapeDtypeStruct(flat, jnp.float32),
        in_specs=[pl.BlockSpec(memory_space=pltpu.VMEM)] * 3,
        out_specs=pl.BlockSpec(memory_space=pltpu.VMEM),
        scratch_shapes=[pltpu.VMEM(flat, jnp.float32)],
        cost_estimate=pl.CostEstimate(
            flops=12 * blocks * depth * lanes, transcendentals=0, bytes_accessed=12 * blocks * depth * lanes
        ),
    )(moisture.reshape(flat), diffusivity.reshape(flat), rain)
    return wet


def lateral_core(padded_head, padded_cond):
    inner_rows = padded_head.shape[1] - 2
    inner_cols = padded_head.shape[2] - 2
    centre = padded_head[:, 1:-1, 1:-1]
    centre_cond = padded_cond[:, 1:-1, 1:-1]
    flux_total = jnp.zeros_like(centre)
    for row_shift, col_shift in ((0, 1), (2, 1), (1, 0), (1, 2)):
        beside = padded_head[
            :, row_shift : row_shift + inner_rows, col_shift : col_shift + inner_cols
        ]
        beside_cond = padded_cond[
            :, row_shift : row_shift + inner_rows, col_shift : col_shift + inner_cols
        ]
        flux_total = flux_total + 0.5 * (centre_cond + beside_cond) * (beside - centre)
    vertical = 0.5 * (centre_cond[1:] + centre_cond[:-1]) * (centre[1:] - centre[:-1])
    flux_total = (
        flux_total
        + jnp.pad(vertical, ((0, 1), (0, 0), (0, 0)))
        - jnp.pad(vertical, ((1, 0), (0, 0), (0, 0)))
    )
    return centre + flow_rate * flux_total


def turn(x, shift, axis):
    return pltpu.roll(x, shift % x.shape[axis], axis)


def sweep_kernel(both_ref, mask_ref, out_ref, first_ref, second_ref, cond_ref):
    layers = both_ref.shape[0] // 2
    out_rows, out_cols = out_ref.shape[1], out_ref.shape[2]
    keep = mask_ref[...] > 0.5

    def conductances(layer_k, carry):
        here = both_ref[layers + layer_k]
        below = both_ref[layers + jnp.minimum(layer_k + 1, layers - 1)]
        cond_ref[0, layer_k] = 0.5 * (here + turn(here, 1, 0))
        cond_ref[1, layer_k] = 0.5 * (here + turn(here, -1, 0))
        cond_ref[2, layer_k] = 0.5 * (here + turn(here, 1, 1))
        cond_ref[3, layer_k] = 0.5 * (here + turn(here, -1, 1))
        cond_ref[4, layer_k] = 0.5 * (below + here)
        return carry

    lax.fori_loop(0, layers, conductances, 0)

    def sweep(read, write, last):
        def body(layer_k, carry):
            centre, upward = carry
            below = read(jnp.minimum(layer_k + 1, layers - 1))
            flux = cond_ref[0, layer_k] * (turn(centre, 1, 0) - centre)
            flux = flux + cond_ref[1, layer_k] * (turn(centre, -1, 0) - centre)
            flux = flux + cond_ref[2, layer_k] * (turn(centre, 1, 1) - centre)
            flux = flux + cond_ref[3, layer_k] * (turn(centre, -1, 1) - centre)
            downward = jnp.where(
                layer_k < layers - 1, cond_ref[4, layer_k] * (below - centre), 0.0
            )
            flux = flux + downward
            flux = flux - upward
            fresh = centre + flow_rate * flux
            if last:
                moved = turn(turn(fresh, -SWEEPS, 0), -SWEEPS, 1)
                out_ref[layer_k] = moved[:out_rows, :out_cols]
            else:
                write(layer_k, jnp.where(keep, fresh, 0.0))
            return (below, downward)

        start = (read(0), jnp.zeros(mask_ref.shape, jnp.float32))
        lax.fori_loop(0, layers, body, start)

    def reader(ref):
        return lambda layer_k: ref[layer_k]

    def writer(ref):
        def write(layer_k, value):
            ref[layer_k] = value

        return write

    sweep(reader(both_ref), writer(first_ref), False)
    for sweep_k in range(1, SWEEPS):
        source, target = (first_ref, second_ref) if sweep_k % 2 else (second_ref, first_ref)
        sweep(reader(source), writer(target), sweep_k == SWEEPS - 1)


def sweeps(both, mask, tile_shape):
    layers, rows, cols = both.shape[0] // 2, both.shape[1], both.shape[2]
    return pl.pallas_call(
        sweep_kernel,
        out_shape=jax.ShapeDtypeStruct(tile_shape, jnp.float32),
        in_specs=[pl.BlockSpec(memory_space=pltpu.VMEM)] * 2,
        out_specs=pl.BlockSpec(memory_space=pltpu.VMEM),
        scratch_shapes=[
            pltpu.VMEM((layers, rows, cols), jnp.float32),
            pltpu.VMEM((layers, rows, cols), jnp.float32),
            pltpu.VMEM((5, layers, rows, cols), jnp.float32),
        ],
        compiler_params=pltpu.CompilerParams(vmem_limit_bytes=48 * 1024 * 1024),
        cost_estimate=pl.CostEstimate(
            flops=20 * SWEEPS * layers * rows * cols,
            transcendentals=0,
            bytes_accessed=4 * (2 * layers * rows * cols + layers * tile_shape[1] * tile_shape[2]),
        ),
    )(both, mask)


def local(moisture, diffusivity, rain, head, conductivity, tile_ids, offsets, patch_ids, counts):
    highest = lax.Precision.HIGHEST
    block_count = moisture.shape[0]
    tile_count = lax.axis_size("gy")
    capacity = block_count // 2
    tile_rows = head.shape[1]
    tile_cols = head.shape[2]
    wet = column_solve(moisture, diffusivity, rain)
    depth = moisture.shape[1]
    bottom = wet[:, (depth - 1) * tile_cols :]
    drain = diffusivity[:, -1, :] * bottom
    in_use = jnp.arange(block_count, dtype=jnp.int32) < counts[0]
    in_use_f = in_use.astype(jnp.float32)
    to_tile = (
        (tile_ids[:, None] == jnp.arange(tile_count, dtype=jnp.int32)[None, :]) & in_use[:, None]
    ).astype(jnp.int32)
    before = jnp.cumsum(to_tile, axis=0) - to_tile
    slot_of = jnp.sum(before * to_tile, axis=1)
    slot_match = slot_of[None, None, :] == jnp.arange(capacity, dtype=jnp.int32)[None, :, None]
    placing = (to_tile.T[:, None, :] * slot_match).astype(jnp.float32)
    outgoing = jnp.einsum("tcb,bj->tcj", placing, drain, precision=highest)
    out_rows = (
        jnp.einsum("tcb,b->tc", placing, (offsets + 1).astype(jnp.float32), precision=highest) - 1.0
    )
    packed = jnp.concatenate(
        [outgoing, jnp.pad(out_rows, ((0, 0), (0, tile_cols - capacity)))[:, None, :]], axis=1
    )
    arrived = lax.all_to_all(packed, "gy", split_axis=0, concat_axis=0, tiled=True)
    incoming = arrived[:, :capacity, :]
    in_rows = arrived[:, capacity, :capacity]
    slot_total = tile_count * capacity
    landing = (
        in_rows.reshape(1, slot_total) == jnp.arange(tile_rows, dtype=jnp.float32)[:, None]
    ).astype(jnp.float32)
    recharge = jnp.dot(landing, incoming.reshape(slot_total, tile_cols), precision=highest)
    field = head.at[0].add(recharge)
    layers = field.shape[0]
    both = with_halo(
        jnp.concatenate([field, conductivity], axis=0), (("gx", 1), ("gy", 2)), SWEEPS
    )
    row_at = (
        lax.axis_index("gx") * tile_rows - SWEEPS + jnp.arange(tile_rows + 2 * SWEEPS)
    )[:, None]
    col_at = (
        lax.axis_index("gy") * tile_cols - SWEEPS + jnp.arange(tile_cols + 2 * SWEEPS)
    )[None, :]
    inside = (
        (row_at >= 0)
        & (row_at < tile_rows * lax.axis_size("gx"))
        & (col_at >= 0)
        & (col_at < tile_cols * tile_count)
    )
    rows_up = -(-(tile_rows + 2 * SWEEPS) // 8) * 8 - (tile_rows + 2 * SWEEPS)
    cols_up = -(-(tile_cols + 2 * SWEEPS) // 128) * 128 - (tile_cols + 2 * SWEEPS)
    mask = jnp.pad(inside.astype(jnp.float32), ((0, rows_up), (0, cols_up)))
    both = jnp.pad(both, ((0, 0), (0, rows_up), (0, cols_up)))
    field = sweeps(both, mask, head.shape)
    surface = field[0]
    answered = jnp.dot(landing.T, surface, precision=highest).reshape(
        tile_count, capacity, tile_cols
    )
    returned = lax.all_to_all(answered, "gy", split_axis=0, concat_axis=0, tiled=True)
    saturation = jnp.einsum("tcb,tcj->bj", placing, returned, precision=highest)
    new_bottom = bottom + capillary * (saturation - in_use_f[:, None] * bottom)
    moisture_out = jnp.concatenate(
        [wet[:, : (depth - 1) * tile_cols], new_bottom], axis=1
    ).reshape(moisture.shape)
    patch_hot = (patch_ids[None, :] == jnp.arange(PATCH_DEV, dtype=jnp.int32)[:, None]).astype(
        jnp.float32
    )
    patch_sums = jnp.dot(patch_hot, saturation, precision=highest)
    return (field, moisture_out, patch_sums)


def solution(mesh):
    placed = (
        P(("gx", "gy"), None, None),
        P(("gx", "gy"), None, None),
        P(("gx", "gy"), None),
        P(None, "gx", "gy"),
        P(None, "gx", "gy"),
        P(("gx", "gy")),
        P(("gx", "gy")),
        P(("gx", "gy")),
        P(("gx", "gy")),
    )
    return jax.shard_map(
        local,
        mesh=mesh,
        in_specs=placed,
        out_specs=(P(None, "gx", "gy"), P(("gx", "gy"), None, None), P(("gx", "gy"), None)),
        check_vma=False,
    )
```

```python
import jax
import jax.numpy as jnp
from jax import lax
from jax.sharding import PartitionSpec as P
from jax.experimental import pallas as pl
from jax.experimental.pallas import tpu as pltpu
from jax.experimental.layout import Layout, with_layout_constraint

PATCH_DEV = 8
SWEEPS = 6


flow_rate = 0.15
capillary = 0.5


def with_halo(cells, sides, width):
    for axis, dim in sides:
        count = lax.axis_size(axis)
        ends = count - 1
        head = lax.slice_in_dim(cells, 0, width, axis=dim)
        tail = lax.slice_in_dim(cells, cells.shape[dim] - width, cells.shape[dim], axis=dim)
        cells = jnp.concatenate(
            [
                lax.ppermute(tail, axis, [(i, (i + 1) % count) for i in range(ends)]),
                cells,
                lax.ppermute(head, axis, [((i + 1) % count, i) for i in range(ends)]),
            ],
            axis=dim,
        )
    return cells


def column_kernel(moist_ref, diff_ref, rain_ref, wet_ref, ratio_ref):
    lanes = rain_ref.shape[1]
    depth = moist_ref.shape[1] // lanes
    group = 8

    def layer(ref, rows, k):
        return ref[rows, k * lanes : (k + 1) * lanes]

    def body(g, carry):
        rows = pl.ds(pl.multiple_of(g * group, group), group)
        ratio = None
        carried = None
        for layer_k in range(depth):
            lower_coef = layer(diff_ref, rows, layer_k)
            source = layer(moist_ref, rows, layer_k)
            if layer_k == 0:
                source = source + rain_ref[rows, :]
                pivot = 1.0 + lower_coef
                carried = source / pivot
            else:
                upper_coef = layer(diff_ref, rows, layer_k - 1)
                pivot = 1.0 + lower_coef + upper_coef - upper_coef * ratio
                carried = (source + upper_coef * carried) / pivot
            ratio = lower_coef / pivot
            ratio_ref[rows, layer_k * lanes : (layer_k + 1) * lanes] = ratio
            wet_ref[rows, layer_k * lanes : (layer_k + 1) * lanes] = carried
        solved = carried
        for layer_k in range(depth - 2, -1, -1):
            solved = layer(wet_ref, rows, layer_k) + layer(ratio_ref, rows, layer_k) * solved
            wet_ref[rows, layer_k * lanes : (layer_k + 1) * lanes] = solved
        return carry

    lax.fori_loop(0, moist_ref.shape[0] // group, body, 0)


def column_solve(moisture, diffusivity, rain):
    blocks, depth, lanes = moisture.shape
    flat = (blocks, depth * lanes)
    wet = pl.pallas_call(
        column_kernel,
        out_shape=jax.ShapeDtypeStruct(flat, jnp.float32),
        in_specs=[pl.BlockSpec(memory_space=pltpu.VMEM)] * 3,
        out_specs=pl.BlockSpec(memory_space=pltpu.VMEM),
        scratch_shapes=[pltpu.VMEM(flat, jnp.float32)],
        cost_estimate=pl.CostEstimate(
            flops=12 * blocks * depth * lanes, transcendentals=0, bytes_accessed=12 * blocks * depth * lanes
        ),
    )(moisture.reshape(flat), diffusivity.reshape(flat), rain)
    return wet


def lateral_core(padded_head, padded_cond):
    inner_rows = padded_head.shape[1] - 2
    inner_cols = padded_head.shape[2] - 2
    centre = padded_head[:, 1:-1, 1:-1]
    centre_cond = padded_cond[:, 1:-1, 1:-1]
    flux_total = jnp.zeros_like(centre)
    for row_shift, col_shift in ((0, 1), (2, 1), (1, 0), (1, 2)):
        beside = padded_head[
            :, row_shift : row_shift + inner_rows, col_shift : col_shift + inner_cols
        ]
        beside_cond = padded_cond[
            :, row_shift : row_shift + inner_rows, col_shift : col_shift + inner_cols
        ]
        flux_total = flux_total + 0.5 * (centre_cond + beside_cond) * (beside - centre)
    vertical = 0.5 * (centre_cond[1:] + centre_cond[:-1]) * (centre[1:] - centre[:-1])
    flux_total = (
        flux_total
        + jnp.pad(vertical, ((0, 1), (0, 0), (0, 0)))
        - jnp.pad(vertical, ((1, 0), (0, 0), (0, 0)))
    )
    return centre + flow_rate * flux_total


def local(moisture, diffusivity, rain, head, conductivity, tile_ids, offsets, patch_ids, counts):
    highest = lax.Precision.HIGHEST
    block_count = moisture.shape[0]
    tile_count = lax.axis_size("gy")
    capacity = block_count // 2
    tile_rows = head.shape[1]
    tile_cols = head.shape[2]
    wet = column_solve(moisture, diffusivity, rain)
    depth = moisture.shape[1]
    bottom = wet[:, (depth - 1) * tile_cols :]
    drain = diffusivity[:, -1, :] * bottom
    in_use = jnp.arange(block_count, dtype=jnp.int32) < counts[0]
    in_use_f = in_use.astype(jnp.float32)
    to_tile = (
        (tile_ids[:, None] == jnp.arange(tile_count, dtype=jnp.int32)[None, :]) & in_use[:, None]
    ).astype(jnp.int32)
    before = jnp.cumsum(to_tile, axis=0) - to_tile
    slot_of = jnp.sum(before * to_tile, axis=1)
    slot_match = slot_of[None, None, :] == jnp.arange(capacity, dtype=jnp.int32)[None, :, None]
    placing = (to_tile.T[:, None, :] * slot_match).astype(jnp.float32)
    outgoing = jnp.einsum("tcb,bj->tcj", placing, drain, precision=highest)
    out_rows = (
        jnp.einsum("tcb,b->tc", placing, (offsets + 1).astype(jnp.float32), precision=highest) - 1.0
    )
    packed = jnp.concatenate(
        [outgoing, jnp.pad(out_rows, ((0, 0), (0, tile_cols - capacity)))[:, None, :]], axis=1
    )
    arrived = lax.all_to_all(packed, "gy", split_axis=0, concat_axis=0, tiled=True)
    incoming = arrived[:, :capacity, :]
    in_rows = arrived[:, capacity, :capacity]
    slot_total = tile_count * capacity
    landing = (
        in_rows.reshape(1, slot_total) == jnp.arange(tile_rows, dtype=jnp.float32)[:, None]
    ).astype(jnp.float32)
    recharge = jnp.dot(landing, incoming.reshape(slot_total, tile_cols), precision=highest)
    field = head.at[0].add(recharge)
    layers = field.shape[0]
    stacked = jnp.concatenate([field, conductivity], axis=0)
    rowed = with_halo(stacked, (("gx", 1),), SWEEPS)
    halo_rows = rowed.shape[1]
    tiled_rows = -(-halo_rows // 8) * 8
    flat = jnp.pad(rowed, ((0, 0), (0, tiled_rows - halo_rows), (0, 0))).reshape(-1, tile_cols)
    picks = jnp.arange(SWEEPS, dtype=jnp.int32)[:, None]
    lanes = jnp.arange(tile_cols, dtype=jnp.int32)[None, :]
    by_lane = (((1,), (1,)), ((), ()))
    left_strip = lax.dot_general(
        (lanes == picks).astype(jnp.float32), flat, by_lane, precision=highest
    )
    right_strip = lax.dot_general(
        (lanes == tile_cols - SWEEPS + picks).astype(jnp.float32), flat, by_lane, precision=highest
    )
    ends = tile_count - 1
    from_left = lax.ppermute(right_strip, "gy", [(i, i + 1) for i in range(ends)])
    from_right = lax.ppermute(left_strip, "gy", [(i + 1, i) for i in range(ends)])
    width = tile_cols + 2 * SWEEPS
    out_lanes = jnp.arange(width, dtype=jnp.int32)[None, :]
    side = jnp.dot(
        jnp.concatenate([from_left, from_right], axis=0).T,
        jnp.concatenate(
            [out_lanes == picks, out_lanes == tile_cols + SWEEPS + picks], axis=0
        ).astype(jnp.float32),
        precision=highest,
    )
    side = with_layout_constraint(side, Layout((0, 1)))
    middle = jnp.pad(flat, ((0, 0), (SWEEPS, SWEEPS)))
    both = (middle + side).reshape(stacked.shape[0], tiled_rows, width)[:, :halo_rows, :]
    field = both[:layers]
    padded_cond = both[layers:]
    row_at = (
        lax.axis_index("gx") * tile_rows - SWEEPS + jnp.arange(tile_rows + 2 * SWEEPS)
    )[:, None]
    col_at = (
        lax.axis_index("gy") * tile_cols - SWEEPS + jnp.arange(tile_cols + 2 * SWEEPS)
    )[None, :]
    inside = (
        (row_at >= 0)
        & (row_at < tile_rows * lax.axis_size("gx"))
        & (col_at >= 0)
        & (col_at < tile_cols * tile_count)
    )
    for sweep_k in range(SWEEPS):
        field = lateral_core(field, padded_cond)
        padded_cond = padded_cond[:, 1:-1, 1:-1]
        if sweep_k < SWEEPS - 1:
            edge = sweep_k + 1
            field = jnp.where(inside[None, edge:-edge, edge:-edge], field, 0.0)
    surface = field[0]
    answered = jnp.dot(landing.T, surface, precision=highest).reshape(
        tile_count, capacity, tile_cols
    )
    returned = lax.all_to_all(answered, "gy", split_axis=0, concat_axis=0, tiled=True)
    saturation = jnp.einsum("tcb,tcj->bj", placing, returned, precision=highest)
    new_bottom = bottom + capillary * (saturation - in_use_f[:, None] * bottom)
    moisture_out = jnp.concatenate(
        [wet[:, : (depth - 1) * tile_cols], new_bottom], axis=1
    ).reshape(moisture.shape)
    patch_hot = (patch_ids[None, :] == jnp.arange(PATCH_DEV, dtype=jnp.int32)[:, None]).astype(
        jnp.float32
    )
    patch_sums = jnp.dot(patch_hot, saturation, precision=highest)
    return (field, moisture_out, patch_sums)


def solution(mesh):
    placed = (
        P(("gx", "gy"), None, None),
        P(("gx", "gy"), None, None),
        P(("gx", "gy"), None),
        P(None, "gx", "gy"),
        P(None, "gx", "gy"),
        P(("gx", "gy")),
        P(("gx", "gy")),
        P(("gx", "gy")),
        P(("gx", "gy")),
    )
    return jax.shard_map(
        local,
        mesh=mesh,
        in_specs=placed,
        out_specs=(P(None, "gx", "gy"), P(("gx", "gy"), None, None), P(("gx", "gy"), None)),
        check_vma=False,
    )
```

```python
import jax
import jax.numpy as jnp
from jax import lax
from jax.sharding import PartitionSpec as P
from jax.experimental import pallas as pl
from jax.experimental.pallas import tpu as pltpu
from jax.experimental.layout import Layout, with_layout_constraint

PATCH_DEV = 8
SWEEPS = 6


flow_rate = 0.15
capillary = 0.5


def with_halo(cells, sides, width):
    for axis, dim in sides:
        count = lax.axis_size(axis)
        ends = count - 1
        head = lax.slice_in_dim(cells, 0, width, axis=dim)
        tail = lax.slice_in_dim(cells, cells.shape[dim] - width, cells.shape[dim], axis=dim)
        cells = jnp.concatenate(
            [
                lax.ppermute(tail, axis, [(i, (i + 1) % count) for i in range(ends)]),
                cells,
                lax.ppermute(head, axis, [((i + 1) % count, i) for i in range(ends)]),
            ],
            axis=dim,
        )
    return cells


def column_kernel(moist_ref, diff_ref, rain_ref, wet_ref, ratio_ref):
    lanes = rain_ref.shape[1]
    depth = moist_ref.shape[1] // lanes
    group = 8

    def layer(ref, rows, k):
        return ref[rows, k * lanes : (k + 1) * lanes]

    def body(g, carry):
        rows = pl.ds(pl.multiple_of(g * group, group), group)
        ratio = None
        carried = None
        for layer_k in range(depth):
            lower_coef = layer(diff_ref, rows, layer_k)
            source = layer(moist_ref, rows, layer_k)
            if layer_k == 0:
                source = source + rain_ref[rows, :]
                pivot = 1.0 + lower_coef
                carried = source / pivot
            else:
                upper_coef = layer(diff_ref, rows, layer_k - 1)
                pivot = 1.0 + lower_coef + upper_coef - upper_coef * ratio
                carried = (source + upper_coef * carried) / pivot
            ratio = lower_coef / pivot
            ratio_ref[rows, layer_k * lanes : (layer_k + 1) * lanes] = ratio
            wet_ref[rows, layer_k * lanes : (layer_k + 1) * lanes] = carried
        solved = carried
        for layer_k in range(depth - 2, -1, -1):
            solved = layer(wet_ref, rows, layer_k) + layer(ratio_ref, rows, layer_k) * solved
            wet_ref[rows, layer_k * lanes : (layer_k + 1) * lanes] = solved
        return carry

    lax.fori_loop(0, moist_ref.shape[0] // group, body, 0)


def column_solve(moisture, diffusivity, rain):
    blocks, depth, lanes = moisture.shape
    flat = (blocks, depth * lanes)
    wet = pl.pallas_call(
        column_kernel,
        out_shape=jax.ShapeDtypeStruct(flat, jnp.float32),
        in_specs=[pl.BlockSpec(memory_space=pltpu.VMEM)] * 3,
        out_specs=pl.BlockSpec(memory_space=pltpu.VMEM),
        scratch_shapes=[pltpu.VMEM(flat, jnp.float32)],
        cost_estimate=pl.CostEstimate(
            flops=12 * blocks * depth * lanes, transcendentals=0, bytes_accessed=12 * blocks * depth * lanes
        ),
    )(moisture.reshape(flat), diffusivity.reshape(flat), rain)
    return wet


def lateral_core(padded_head, padded_cond):
    inner_rows = padded_head.shape[1] - 2
    inner_cols = padded_head.shape[2] - 2
    centre = padded_head[:, 1:-1, 1:-1]
    centre_cond = padded_cond[:, 1:-1, 1:-1]
    flux_total = jnp.zeros_like(centre)
    for row_shift, col_shift in ((0, 1), (2, 1), (1, 0), (1, 2)):
        beside = padded_head[
            :, row_shift : row_shift + inner_rows, col_shift : col_shift + inner_cols
        ]
        beside_cond = padded_cond[
            :, row_shift : row_shift + inner_rows, col_shift : col_shift + inner_cols
        ]
        flux_total = flux_total + 0.5 * (centre_cond + beside_cond) * (beside - centre)
    downward = 0.5 * (centre_cond[1:] + centre_cond[:-1]) * (centre[1:] - centre[:-1])
    upward = 0.5 * (centre_cond[:-1] + centre_cond[1:]) * (centre[1:] - centre[:-1])
    flux_total = (
        flux_total
        + jnp.pad(downward, ((0, 1), (0, 0), (0, 0)))
        - jnp.pad(upward, ((1, 0), (0, 0), (0, 0)))
    )
    return centre + flow_rate * flux_total


def exchange(chunks, axis):
    count = lax.axis_size(axis)
    me = lax.axis_index(axis)
    own = lax.dynamic_index_in_dim(chunks, me, axis=0, keepdims=False)
    got = [own]
    for shift in range(1, count):
        outgoing = lax.dynamic_index_in_dim(chunks, (me + shift) % count, axis=0, keepdims=False)
        got.append(lax.ppermute(outgoing, axis, [(i, (i + shift) % count) for i in range(count)]))
    placed = []
    for source in range(count):
        distance = (me - source) % count
        pick = got[0]
        for shift in range(1, count):
            pick = jnp.where(distance == shift, got[shift], pick)
        placed.append(pick)
    return jnp.stack(placed)


def local(moisture, diffusivity, rain, head, conductivity, tile_ids, offsets, patch_ids, counts):
    highest = lax.Precision.HIGHEST
    block_count = moisture.shape[0]
    tile_count = lax.axis_size("gy")
    capacity = block_count // 2
    tile_rows = head.shape[1]
    tile_cols = head.shape[2]
    wet = column_solve(moisture, diffusivity, rain)
    depth = moisture.shape[1]
    bottom = wet[:, (depth - 1) * tile_cols :]
    drain = diffusivity[:, -1, :] * bottom
    in_use = jnp.arange(block_count, dtype=jnp.int32) < counts[0]
    in_use_f = in_use.astype(jnp.float32)
    to_tile = (
        (tile_ids[:, None] == jnp.arange(tile_count, dtype=jnp.int32)[None, :]) & in_use[:, None]
    ).astype(jnp.int32)
    before = jnp.cumsum(to_tile, axis=0) - to_tile
    slot_of = jnp.sum(before * to_tile, axis=1)
    slot_match = slot_of[None, None, :] == jnp.arange(capacity, dtype=jnp.int32)[None, :, None]
    placing = (to_tile.T[:, None, :] * slot_match).astype(jnp.float32)
    outgoing = jnp.einsum("tcb,bj->tcj", placing, drain, precision=highest)
    out_rows = (
        jnp.einsum("tcb,b->tc", placing, (offsets + 1).astype(jnp.float32), precision=highest) - 1.0
    )
    packed = jnp.concatenate(
        [outgoing, jnp.pad(out_rows, ((0, 0), (0, tile_cols - capacity)))[:, None, :]], axis=1
    )
    arrived = exchange(packed, "gy")
    incoming = arrived[:, :capacity, :]
    in_rows = arrived[:, capacity, :capacity]
    slot_total = tile_count * capacity
    landing = (
        in_rows.reshape(1, slot_total) == jnp.arange(tile_rows, dtype=jnp.float32)[:, None]
    ).astype(jnp.float32)
    recharge = jnp.dot(landing, incoming.reshape(slot_total, tile_cols), precision=highest)
    field = head.at[0].add(recharge)
    layers = field.shape[0]
    stacked = jnp.concatenate([field, conductivity], axis=0)
    rowed = with_halo(stacked, (("gx", 1),), SWEEPS)
    halo_rows = rowed.shape[1]
    tiled_rows = -(-halo_rows // 8) * 8
    flat = jnp.pad(rowed, ((0, 0), (0, tiled_rows - halo_rows), (0, 0))).reshape(-1, tile_cols)
    picks = jnp.arange(SWEEPS, dtype=jnp.int32)[:, None]
    lanes = jnp.arange(tile_cols, dtype=jnp.int32)[None, :]
    by_lane = (((1,), (1,)), ((), ()))
    left_strip = lax.dot_general(
        (lanes == picks).astype(jnp.float32), flat, by_lane, precision=highest
    )
    right_strip = lax.dot_general(
        (lanes == tile_cols - SWEEPS + picks).astype(jnp.float32), flat, by_lane, precision=highest
    )
    ends = tile_count - 1
    from_left = lax.ppermute(right_strip, "gy", [(i, i + 1) for i in range(ends)])
    from_right = lax.ppermute(left_strip, "gy", [(i + 1, i) for i in range(ends)])
    width = tile_cols + 2 * SWEEPS
    out_lanes = jnp.arange(width, dtype=jnp.int32)[None, :]
    side = jnp.dot(
        jnp.concatenate([from_left, from_right], axis=0).T,
        jnp.concatenate(
            [out_lanes == picks, out_lanes == tile_cols + SWEEPS + picks], axis=0
        ).astype(jnp.float32),
        precision=highest,
    )
    side = with_layout_constraint(side, Layout((0, 1)))
    middle = jnp.pad(flat, ((0, 0), (SWEEPS, SWEEPS)))
    both = (middle + side).reshape(stacked.shape[0], tiled_rows, width)[:, :halo_rows, :]
    field = both[:layers]
    padded_cond = both[layers:]
    row_at = (
        lax.axis_index("gx") * tile_rows - SWEEPS + jnp.arange(tile_rows + 2 * SWEEPS)
    )[:, None]
    col_at = (
        lax.axis_index("gy") * tile_cols - SWEEPS + jnp.arange(tile_cols + 2 * SWEEPS)
    )[None, :]
    inside = (
        (row_at >= 0)
        & (row_at < tile_rows * lax.axis_size("gx"))
        & (col_at >= 0)
        & (col_at < tile_cols * tile_count)
    )
    for sweep_k in range(SWEEPS):
        field = lateral_core(field, padded_cond)
        padded_cond = padded_cond[:, 1:-1, 1:-1]
        if sweep_k < SWEEPS - 1:
            edge = sweep_k + 1
            field = jnp.where(inside[None, edge:-edge, edge:-edge], field, 0.0)
    surface = field[0]
    answered = jnp.dot(landing.T, surface, precision=highest).reshape(
        tile_count, capacity, tile_cols
    )
    returned = exchange(answered, "gy")
    saturation = jnp.einsum("tcb,tcj->bj", placing, returned, precision=highest)
    new_bottom = bottom + capillary * (saturation - in_use_f[:, None] * bottom)
    moisture_out = jnp.concatenate(
        [wet[:, : (depth - 1) * tile_cols], new_bottom], axis=1
    ).reshape(moisture.shape)
    patch_hot = (patch_ids[None, :] == jnp.arange(PATCH_DEV, dtype=jnp.int32)[:, None]).astype(
        jnp.float32
    )
    patch_sums = jnp.dot(patch_hot, saturation, precision=highest)
    return (field, moisture_out, patch_sums)


def solution(mesh):
    placed = (
        P(("gx", "gy"), None, None),
        P(("gx", "gy"), None, None),
        P(("gx", "gy"), None),
        P(None, "gx", "gy"),
        P(None, "gx", "gy"),
        P(("gx", "gy")),
        P(("gx", "gy")),
        P(("gx", "gy")),
        P(("gx", "gy")),
    )
    return jax.shard_map(
        local,
        mesh=mesh,
        in_specs=placed,
        out_specs=(P(None, "gx", "gy"), P(("gx", "gy"), None, None), P(("gx", "gy"), None)),
        check_vma=False,
    )
```

```python
import jax
import jax.numpy as jnp
from jax import lax
from jax.sharding import PartitionSpec as P
from jax.experimental import pallas as pl
from jax.experimental.pallas import tpu as pltpu
from jax.experimental.layout import Layout, with_layout_constraint

PATCH_DEV = 8
SWEEPS = 6


flow_rate = 0.15
capillary = 0.5


def with_halo(cells, sides, width):
    for axis, dim in sides:
        count = lax.axis_size(axis)
        ends = count - 1
        head = lax.slice_in_dim(cells, 0, width, axis=dim)
        tail = lax.slice_in_dim(cells, cells.shape[dim] - width, cells.shape[dim], axis=dim)
        cells = jnp.concatenate(
            [
                lax.ppermute(tail, axis, [(i, (i + 1) % count) for i in range(ends)]),
                cells,
                lax.ppermute(head, axis, [((i + 1) % count, i) for i in range(ends)]),
            ],
            axis=dim,
        )
    return cells


def column_kernel(moist_ref, diff_ref, rain_ref, wet_ref, ratio_ref):
    depth = moist_ref.shape[0]
    group = 8

    def body(g, carry):
        rows = pl.ds(pl.multiple_of(g * group, group), group)
        ratio = None
        carried = None
        for layer_k in range(depth):
            lower_coef = diff_ref[layer_k, rows, :]
            source = moist_ref[layer_k, rows, :]
            if layer_k == 0:
                source = source + rain_ref[rows, :]
                pivot = 1.0 + lower_coef
                carried = source / pivot
            else:
                upper_coef = diff_ref[layer_k - 1, rows, :]
                pivot = 1.0 + lower_coef + upper_coef - upper_coef * ratio
                carried = (source + upper_coef * carried) / pivot
            ratio = lower_coef / pivot
            ratio_ref[layer_k, rows, :] = ratio
            wet_ref[layer_k, rows, :] = carried
        solved = carried
        for layer_k in range(depth - 2, -1, -1):
            solved = wet_ref[layer_k, rows, :] + ratio_ref[layer_k, rows, :] * solved
            wet_ref[layer_k, rows, :] = solved
        return carry

    lax.fori_loop(0, moist_ref.shape[1] // group, body, 0)


def column_solve(moisture, diffusivity, rain):
    blocks, depth, lanes = moisture.shape
    layered = (depth, blocks, lanes)
    return pl.pallas_call(
        column_kernel,
        out_shape=jax.ShapeDtypeStruct(layered, jnp.float32),
        in_specs=[pl.BlockSpec(memory_space=pltpu.VMEM)] * 3,
        out_specs=pl.BlockSpec(memory_space=pltpu.VMEM),
        scratch_shapes=[pltpu.VMEM(layered, jnp.float32)],
        cost_estimate=pl.CostEstimate(
            flops=12 * blocks * depth * lanes, transcendentals=0, bytes_accessed=12 * blocks * depth * lanes
        ),
    )(jnp.transpose(moisture, (1, 0, 2)), jnp.transpose(diffusivity, (1, 0, 2)), rain)


def lateral_core(padded_head, padded_cond):
    inner_rows = padded_head.shape[1] - 2
    inner_cols = padded_head.shape[2] - 2
    centre = padded_head[:, 1:-1, 1:-1]
    centre_cond = padded_cond[:, 1:-1, 1:-1]
    flux_total = jnp.zeros_like(centre)
    for row_shift, col_shift in ((0, 1), (2, 1), (1, 0), (1, 2)):
        beside = padded_head[
            :, row_shift : row_shift + inner_rows, col_shift : col_shift + inner_cols
        ]
        beside_cond = padded_cond[
            :, row_shift : row_shift + inner_rows, col_shift : col_shift + inner_cols
        ]
        flux_total = flux_total + 0.5 * (centre_cond + beside_cond) * (beside - centre)
    vertical = 0.5 * (centre_cond[1:] + centre_cond[:-1]) * (centre[1:] - centre[:-1])
    flux_total = (
        flux_total
        + jnp.pad(vertical, ((0, 1), (0, 0), (0, 0)))
        - jnp.pad(vertical, ((1, 0), (0, 0), (0, 0)))
    )
    return centre + flow_rate * flux_total


def local(moisture, diffusivity, rain, head, conductivity, tile_ids, offsets, patch_ids, counts):
    highest = lax.Precision.HIGHEST
    block_count = moisture.shape[0]
    tile_count = lax.axis_size("gy")
    capacity = block_count // 2
    tile_rows = head.shape[1]
    tile_cols = head.shape[2]
    wet = column_solve(moisture, diffusivity, rain)
    depth = moisture.shape[1]
    bottom = wet[depth - 1]
    drain = diffusivity[:, -1, :] * bottom
    in_use = jnp.arange(block_count, dtype=jnp.int32) < counts[0]
    in_use_f = in_use.astype(jnp.float32)
    to_tile = (
        (tile_ids[:, None] == jnp.arange(tile_count, dtype=jnp.int32)[None, :]) & in_use[:, None]
    ).astype(jnp.int32)
    before = jnp.cumsum(to_tile, axis=0) - to_tile
    slot_of = jnp.sum(before * to_tile, axis=1)
    slot_match = slot_of[None, None, :] == jnp.arange(capacity, dtype=jnp.int32)[None, :, None]
    placing = (to_tile.T[:, None, :] * slot_match).astype(jnp.float32)
    outgoing = jnp.einsum("tcb,bj->tcj", placing, drain, precision=highest)
    out_rows = (
        jnp.einsum("tcb,b->tc", placing, (offsets + 1).astype(jnp.float32), precision=highest) - 1.0
    )
    packed = jnp.concatenate(
        [outgoing, jnp.pad(out_rows, ((0, 0), (0, tile_cols - capacity)))[:, None, :]], axis=1
    )
    arrived = lax.all_to_all(packed, "gy", split_axis=0, concat_axis=0, tiled=True)
    incoming = arrived[:, :capacity, :]
    in_rows = arrived[:, capacity, :capacity]
    slot_total = tile_count * capacity
    landing = (
        in_rows.reshape(1, slot_total) == jnp.arange(tile_rows, dtype=jnp.float32)[:, None]
    ).astype(jnp.float32)
    recharge = jnp.dot(landing, incoming.reshape(slot_total, tile_cols), precision=highest)
    field = head.at[0].add(recharge)
    layers = field.shape[0]
    stacked = jnp.concatenate([field, conductivity], axis=0)
    rowed = with_halo(stacked, (("gx", 1),), SWEEPS)
    halo_rows = rowed.shape[1]
    tiled_rows = -(-halo_rows // 8) * 8
    flat = jnp.pad(rowed, ((0, 0), (0, tiled_rows - halo_rows), (0, 0))).reshape(-1, tile_cols)
    picks = jnp.arange(SWEEPS, dtype=jnp.int32)[:, None]
    lanes = jnp.arange(tile_cols, dtype=jnp.int32)[None, :]
    by_lane = (((1,), (1,)), ((), ()))
    left_strip = lax.dot_general(
        (lanes == picks).astype(jnp.float32), flat, by_lane, precision=highest
    )
    right_strip = lax.dot_general(
        (lanes == tile_cols - SWEEPS + picks).astype(jnp.float32), flat, by_lane, precision=highest
    )
    ends = tile_count - 1
    from_left = lax.ppermute(right_strip, "gy", [(i, i + 1) for i in range(ends)])
    from_right = lax.ppermute(left_strip, "gy", [(i + 1, i) for i in range(ends)])
    width = tile_cols + 2 * SWEEPS
    out_lanes = jnp.arange(width, dtype=jnp.int32)[None, :]
    side = jnp.dot(
        jnp.concatenate([from_left, from_right], axis=0).T,
        jnp.concatenate(
            [out_lanes == picks, out_lanes == tile_cols + SWEEPS + picks], axis=0
        ).astype(jnp.float32),
        precision=highest,
    )
    side = with_layout_constraint(side, Layout((0, 1)))
    middle = jnp.pad(flat, ((0, 0), (SWEEPS, SWEEPS)))
    both = (middle + side).reshape(stacked.shape[0], tiled_rows, width)[:, :halo_rows, :]
    field = both[:layers]
    padded_cond = both[layers:]
    row_at = (
        lax.axis_index("gx") * tile_rows - SWEEPS + jnp.arange(tile_rows + 2 * SWEEPS)
    )[:, None]
    col_at = (
        lax.axis_index("gy") * tile_cols - SWEEPS + jnp.arange(tile_cols + 2 * SWEEPS)
    )[None, :]
    inside = (
        (row_at >= 0)
        & (row_at < tile_rows * lax.axis_size("gx"))
        & (col_at >= 0)
        & (col_at < tile_cols * tile_count)
    )
    for sweep_k in range(SWEEPS):
        field = lateral_core(field, padded_cond)
        padded_cond = padded_cond[:, 1:-1, 1:-1]
        if sweep_k < SWEEPS - 1:
            edge = sweep_k + 1
            field = jnp.where(inside[None, edge:-edge, edge:-edge], field, 0.0)
    surface = field[0]
    answered = jnp.dot(landing.T, surface, precision=highest).reshape(
        tile_count, capacity, tile_cols
    )
    returned = lax.all_to_all(answered, "gy", split_axis=0, concat_axis=0, tiled=True)
    saturation = jnp.einsum("tcb,tcj->bj", placing, returned, precision=highest)
    new_bottom = bottom + capillary * (saturation - in_use_f[:, None] * bottom)
    moisture_out = jnp.transpose(jnp.concatenate([wet[: depth - 1], new_bottom[None]]), (1, 0, 2))
    patch_hot = (patch_ids[None, :] == jnp.arange(PATCH_DEV, dtype=jnp.int32)[:, None]).astype(
        jnp.float32
    )
    patch_sums = jnp.dot(patch_hot, saturation, precision=highest)
    return (field, moisture_out, patch_sums)


def solution(mesh):
    placed = (
        P(("gx", "gy"), None, None),
        P(("gx", "gy"), None, None),
        P(("gx", "gy"), None),
        P(None, "gx", "gy"),
        P(None, "gx", "gy"),
        P(("gx", "gy")),
        P(("gx", "gy")),
        P(("gx", "gy")),
        P(("gx", "gy")),
    )
    return jax.shard_map(
        local,
        mesh=mesh,
        in_specs=placed,
        out_specs=(P(None, "gx", "gy"), P(("gx", "gy"), None, None), P(("gx", "gy"), None)),
        check_vma=False,
    )
```

```python
import jax
import jax.numpy as jnp
from jax import lax
from jax.sharding import PartitionSpec as P
from jax.experimental import pallas as pl
from jax.experimental.pallas import tpu as pltpu
from jax.experimental.layout import Layout, with_layout_constraint

PATCH_DEV = 8
SWEEPS = 6


flow_rate = 0.15
capillary = 0.5


def with_halo(cells, sides, width):
    for axis, dim in sides:
        count = lax.axis_size(axis)
        ends = count - 1
        head = lax.slice_in_dim(cells, 0, width, axis=dim)
        tail = lax.slice_in_dim(cells, cells.shape[dim] - width, cells.shape[dim], axis=dim)
        cells = jnp.concatenate(
            [
                lax.ppermute(tail, axis, [(i, (i + 1) % count) for i in range(ends)]),
                cells,
                lax.ppermute(head, axis, [((i + 1) % count, i) for i in range(ends)]),
            ],
            axis=dim,
        )
    return cells


def column_kernel(moist_ref, diff_ref, rain_ref, wet_ref, ratio_ref):
    depth = moist_ref.shape[0]

    def body(g, carry):
        rows = pl.ds(0, moist_ref.shape[1])
        ratio = None
        carried = None
        for layer_k in range(depth):
            lower_coef = diff_ref[layer_k, rows, :]
            source = moist_ref[layer_k, rows, :]
            if layer_k == 0:
                source = source + rain_ref[rows, :]
                pivot = 1.0 + lower_coef
                carried = source / pivot
            else:
                upper_coef = diff_ref[layer_k - 1, rows, :]
                pivot = 1.0 + lower_coef + upper_coef - upper_coef * ratio
                carried = (source + upper_coef * carried) / pivot
            ratio = lower_coef / pivot
            ratio_ref[layer_k, rows, :] = ratio
            wet_ref[layer_k, rows, :] = carried
        solved = carried
        for layer_k in range(depth - 2, -1, -1):
            solved = wet_ref[layer_k, rows, :] + ratio_ref[layer_k, rows, :] * solved
            wet_ref[layer_k, rows, :] = solved
        return carry

    body(0, 0)


def column_solve(moisture, diffusivity, rain):
    blocks, depth, lanes = moisture.shape
    layered = (depth, blocks, lanes)
    return pl.pallas_call(
        column_kernel,
        out_shape=jax.ShapeDtypeStruct(layered, jnp.float32),
        in_specs=[pl.BlockSpec(memory_space=pltpu.VMEM)] * 3,
        out_specs=pl.BlockSpec(memory_space=pltpu.VMEM),
        scratch_shapes=[pltpu.VMEM(layered, jnp.float32)],
        cost_estimate=pl.CostEstimate(
            flops=12 * blocks * depth * lanes, transcendentals=0, bytes_accessed=12 * blocks * depth * lanes
        ),
    )(jnp.transpose(moisture, (1, 0, 2)), jnp.transpose(diffusivity, (1, 0, 2)), rain)


def lateral_core(padded_head, padded_cond):
    inner_rows = padded_head.shape[1] - 2
    inner_cols = padded_head.shape[2] - 2
    centre = padded_head[:, 1:-1, 1:-1]
    centre_cond = padded_cond[:, 1:-1, 1:-1]
    flux_total = jnp.zeros_like(centre)
    for row_shift, col_shift in ((0, 1), (2, 1), (1, 0), (1, 2)):
        beside = padded_head[
            :, row_shift : row_shift + inner_rows, col_shift : col_shift + inner_cols
        ]
        beside_cond = padded_cond[
            :, row_shift : row_shift + inner_rows, col_shift : col_shift + inner_cols
        ]
        flux_total = flux_total + 0.5 * (centre_cond + beside_cond) * (beside - centre)
    vertical = 0.5 * (centre_cond[1:] + centre_cond[:-1]) * (centre[1:] - centre[:-1])
    flux_total = (
        flux_total
        + jnp.pad(vertical, ((0, 1), (0, 0), (0, 0)))
        - jnp.pad(vertical, ((1, 0), (0, 0), (0, 0)))
    )
    return centre + flow_rate * flux_total


def local(moisture, diffusivity, rain, head, conductivity, tile_ids, offsets, patch_ids, counts):
    highest = lax.Precision.HIGHEST
    block_count = moisture.shape[0]
    tile_count = lax.axis_size("gy")
    capacity = block_count // 2
    tile_rows = head.shape[1]
    tile_cols = head.shape[2]
    wet = column_solve(moisture, diffusivity, rain)
    depth = moisture.shape[1]
    bottom = wet[depth - 1]
    drain = diffusivity[:, -1, :] * bottom
    in_use = jnp.arange(block_count, dtype=jnp.int32) < counts[0]
    in_use_f = in_use.astype(jnp.float32)
    to_tile = (
        (tile_ids[:, None] == jnp.arange(tile_count, dtype=jnp.int32)[None, :]) & in_use[:, None]
    ).astype(jnp.int32)
    before = jnp.cumsum(to_tile, axis=0) - to_tile
    slot_of = jnp.sum(before * to_tile, axis=1)
    slot_match = slot_of[None, None, :] == jnp.arange(capacity, dtype=jnp.int32)[None, :, None]
    placing = (to_tile.T[:, None, :] * slot_match).astype(jnp.float32)
    outgoing = jnp.einsum("tcb,bj->tcj", placing, drain, precision=highest)
    out_rows = (
        jnp.einsum("tcb,b->tc", placing, (offsets + 1).astype(jnp.float32), precision=highest) - 1.0
    )
    packed = jnp.concatenate(
        [outgoing, jnp.pad(out_rows, ((0, 0), (0, tile_cols - capacity)))[:, None, :]], axis=1
    )
    arrived = lax.all_to_all(packed, "gy", split_axis=0, concat_axis=0, tiled=True)
    incoming = arrived[:, :capacity, :]
    in_rows = arrived[:, capacity, :capacity]
    slot_total = tile_count * capacity
    landing = (
        in_rows.reshape(1, slot_total) == jnp.arange(tile_rows, dtype=jnp.float32)[:, None]
    ).astype(jnp.float32)
    recharge = jnp.dot(landing, incoming.reshape(slot_total, tile_cols), precision=highest)
    field = head.at[0].add(recharge)
    layers = field.shape[0]
    stacked = jnp.concatenate([field, conductivity], axis=0)
    rowed = with_halo(stacked, (("gx", 1),), SWEEPS)
    halo_rows = rowed.shape[1]
    tiled_rows = -(-halo_rows // 8) * 8
    flat = jnp.pad(rowed, ((0, 0), (0, tiled_rows - halo_rows), (0, 0))).reshape(-1, tile_cols)
    picks = jnp.arange(SWEEPS, dtype=jnp.int32)[:, None]
    lanes = jnp.arange(tile_cols, dtype=jnp.int32)[None, :]
    by_lane = (((1,), (1,)), ((), ()))
    left_strip = lax.dot_general(
        (lanes == picks).astype(jnp.float32), flat, by_lane, precision=highest
    )
    right_strip = lax.dot_general(
        (lanes == tile_cols - SWEEPS + picks).astype(jnp.float32), flat, by_lane, precision=highest
    )
    ends = tile_count - 1
    from_left = lax.ppermute(right_strip, "gy", [(i, i + 1) for i in range(ends)])
    from_right = lax.ppermute(left_strip, "gy", [(i + 1, i) for i in range(ends)])
    width = tile_cols + 2 * SWEEPS
    out_lanes = jnp.arange(width, dtype=jnp.int32)[None, :]
    side = jnp.dot(
        jnp.concatenate([from_left, from_right], axis=0).T,
        jnp.concatenate(
            [out_lanes == picks, out_lanes == tile_cols + SWEEPS + picks], axis=0
        ).astype(jnp.float32),
        precision=highest,
    )
    side = with_layout_constraint(side, Layout((0, 1)))
    middle = jnp.pad(flat, ((0, 0), (SWEEPS, SWEEPS)))
    both = (middle + side).reshape(stacked.shape[0], tiled_rows, width)[:, :halo_rows, :]
    field = both[:layers]
    padded_cond = both[layers:]
    row_at = (
        lax.axis_index("gx") * tile_rows - SWEEPS + jnp.arange(tile_rows + 2 * SWEEPS)
    )[:, None]
    col_at = (
        lax.axis_index("gy") * tile_cols - SWEEPS + jnp.arange(tile_cols + 2 * SWEEPS)
    )[None, :]
    inside = (
        (row_at >= 0)
        & (row_at < tile_rows * lax.axis_size("gx"))
        & (col_at >= 0)
        & (col_at < tile_cols * tile_count)
    )
    for sweep_k in range(SWEEPS):
        field = lateral_core(field, padded_cond)
        padded_cond = padded_cond[:, 1:-1, 1:-1]
        if sweep_k < SWEEPS - 1:
            edge = sweep_k + 1
            field = jnp.where(inside[None, edge:-edge, edge:-edge], field, 0.0)
    surface = field[0]
    answered = jnp.dot(landing.T, surface, precision=highest).reshape(
        tile_count, capacity, tile_cols
    )
    returned = lax.all_to_all(answered, "gy", split_axis=0, concat_axis=0, tiled=True)
    saturation = jnp.einsum("tcb,tcj->bj", placing, returned, precision=highest)
    new_bottom = bottom + capillary * (saturation - in_use_f[:, None] * bottom)
    moisture_out = jnp.transpose(jnp.concatenate([wet[: depth - 1], new_bottom[None]]), (1, 0, 2))
    patch_hot = (patch_ids[None, :] == jnp.arange(PATCH_DEV, dtype=jnp.int32)[:, None]).astype(
        jnp.float32
    )
    patch_sums = jnp.dot(patch_hot, saturation, precision=highest)
    return (field, moisture_out, patch_sums)


def solution(mesh):
    placed = (
        P(("gx", "gy"), None, None),
        P(("gx", "gy"), None, None),
        P(("gx", "gy"), None),
        P(None, "gx", "gy"),
        P(None, "gx", "gy"),
        P(("gx", "gy")),
        P(("gx", "gy")),
        P(("gx", "gy")),
        P(("gx", "gy")),
    )
    return jax.shard_map(
        local,
        mesh=mesh,
        in_specs=placed,
        out_specs=(P(None, "gx", "gy"), P(("gx", "gy"), None, None), P(("gx", "gy"), None)),
        check_vma=False,
    )
```

```python
import jax
import jax.numpy as jnp
from jax import lax
from jax.sharding import PartitionSpec as P
from jax.experimental import pallas as pl
from jax.experimental.pallas import tpu as pltpu
from jax.experimental.layout import Layout, with_layout_constraint

PATCH_DEV = 8
SWEEPS = 6


flow_rate = 0.15
capillary = 0.5


def with_halo(cells, sides, width):
    for axis, dim in sides:
        count = lax.axis_size(axis)
        ends = count - 1
        head = lax.slice_in_dim(cells, 0, width, axis=dim)
        tail = lax.slice_in_dim(cells, cells.shape[dim] - width, cells.shape[dim], axis=dim)
        cells = jnp.concatenate(
            [
                lax.ppermute(tail, axis, [(i, (i + 1) % count) for i in range(ends)]),
                cells,
                lax.ppermute(head, axis, [((i + 1) % count, i) for i in range(ends)]),
            ],
            axis=dim,
        )
    return cells


def column_kernel(moist_ref, diff_ref, rain_ref, wet_ref, ratio_ref):
    depth = moist_ref.shape[0]

    def body(g, carry):
        rows = pl.ds(0, moist_ref.shape[1])
        ratio = None
        carried = None
        for layer_k in range(depth):
            lower_coef = diff_ref[layer_k, rows, :]
            source = moist_ref[layer_k, rows, :]
            if layer_k == 0:
                source = source + rain_ref[rows, :]
                pivot = 1.0 + lower_coef
                carried = source / pivot
            else:
                upper_coef = diff_ref[layer_k - 1, rows, :]
                pivot = 1.0 + lower_coef + upper_coef - upper_coef * ratio
                carried = (source + upper_coef * carried) / pivot
            ratio = lower_coef / pivot
            ratio_ref[layer_k, rows, :] = ratio
            wet_ref[layer_k, rows, :] = carried
        solved = carried
        for layer_k in range(depth - 2, -1, -1):
            solved = wet_ref[layer_k, rows, :] + ratio_ref[layer_k, rows, :] * solved
            wet_ref[layer_k, rows, :] = solved
        return carry

    body(0, 0)


def column_solve(moisture, diffusivity, rain):
    blocks, depth, lanes = moisture.shape
    layered = (depth, blocks, lanes)
    return pl.pallas_call(
        column_kernel,
        out_shape=jax.ShapeDtypeStruct(layered, jnp.float32),
        in_specs=[pl.BlockSpec(memory_space=pltpu.VMEM)] * 3,
        out_specs=pl.BlockSpec(memory_space=pltpu.VMEM),
        scratch_shapes=[pltpu.VMEM(layered, jnp.float32)],
        cost_estimate=pl.CostEstimate(
            flops=12 * blocks * depth * lanes, transcendentals=0, bytes_accessed=12 * blocks * depth * lanes
        ),
    )(jnp.transpose(moisture, (1, 0, 2)), jnp.transpose(diffusivity, (1, 0, 2)), rain)


SHIFTS = ((0, 1), (2, 1), (1, 0), (1, 2))


def conductances(padded_cond):
    inner_rows = padded_cond.shape[1] - 2
    inner_cols = padded_cond.shape[2] - 2
    centre_cond = padded_cond[:, 1:-1, 1:-1]
    sides = []
    for row_shift, col_shift in SHIFTS:
        beside_cond = padded_cond[
            :, row_shift : row_shift + inner_rows, col_shift : col_shift + inner_cols
        ]
        sides.append(0.5 * (centre_cond + beside_cond))
    sides.append(0.5 * (centre_cond[1:] + centre_cond[:-1]))
    return sides


def lateral_core(padded_head, sides):
    inner_rows = padded_head.shape[1] - 2
    inner_cols = padded_head.shape[2] - 2
    centre = padded_head[:, 1:-1, 1:-1]
    flux_total = jnp.zeros_like(centre)
    for (row_shift, col_shift), side in zip(SHIFTS, sides):
        beside = padded_head[
            :, row_shift : row_shift + inner_rows, col_shift : col_shift + inner_cols
        ]
        flux_total = flux_total + side * (beside - centre)
    vertical = sides[4] * (centre[1:] - centre[:-1])
    flux_total = (
        flux_total
        + jnp.pad(vertical, ((0, 1), (0, 0), (0, 0)))
        - jnp.pad(vertical, ((1, 0), (0, 0), (0, 0)))
    )
    return centre + flow_rate * flux_total


def local(moisture, diffusivity, rain, head, conductivity, tile_ids, offsets, patch_ids, counts):
    highest = lax.Precision.HIGHEST
    block_count = moisture.shape[0]
    tile_count = lax.axis_size("gy")
    capacity = block_count // 2
    tile_rows = head.shape[1]
    tile_cols = head.shape[2]
    wet = column_solve(moisture, diffusivity, rain)
    depth = moisture.shape[1]
    bottom = wet[depth - 1]
    drain = diffusivity[:, -1, :] * bottom
    in_use = jnp.arange(block_count, dtype=jnp.int32) < counts[0]
    in_use_f = in_use.astype(jnp.float32)
    to_tile = (
        (tile_ids[:, None] == jnp.arange(tile_count, dtype=jnp.int32)[None, :]) & in_use[:, None]
    ).astype(jnp.int32)
    before = jnp.cumsum(to_tile, axis=0) - to_tile
    slot_of = jnp.sum(before * to_tile, axis=1)
    slot_match = slot_of[None, None, :] == jnp.arange(capacity, dtype=jnp.int32)[None, :, None]
    placing = (to_tile.T[:, None, :] * slot_match).astype(jnp.float32)
    outgoing = jnp.einsum("tcb,bj->tcj", placing, drain, precision=highest)
    out_rows = (
        jnp.einsum("tcb,b->tc", placing, (offsets + 1).astype(jnp.float32), precision=highest) - 1.0
    )
    packed = jnp.concatenate(
        [outgoing, jnp.pad(out_rows, ((0, 0), (0, tile_cols - capacity)))[:, None, :]], axis=1
    )
    arrived = lax.all_to_all(packed, "gy", split_axis=0, concat_axis=0, tiled=True)
    incoming = arrived[:, :capacity, :]
    in_rows = arrived[:, capacity, :capacity]
    slot_total = tile_count * capacity
    landing = (
        in_rows.reshape(1, slot_total) == jnp.arange(tile_rows, dtype=jnp.float32)[:, None]
    ).astype(jnp.float32)
    recharge = jnp.dot(landing, incoming.reshape(slot_total, tile_cols), precision=highest)
    field = head.at[0].add(recharge)
    layers = field.shape[0]
    stacked = jnp.concatenate([field, conductivity], axis=0)
    rowed = with_halo(stacked, (("gx", 1),), SWEEPS)
    halo_rows = rowed.shape[1]
    tiled_rows = -(-halo_rows // 8) * 8
    flat = jnp.pad(rowed, ((0, 0), (0, tiled_rows - halo_rows), (0, 0))).reshape(-1, tile_cols)
    picks = jnp.arange(SWEEPS, dtype=jnp.int32)[:, None]
    lanes = jnp.arange(tile_cols, dtype=jnp.int32)[None, :]
    by_lane = (((1,), (1,)), ((), ()))
    left_strip = lax.dot_general(
        (lanes == picks).astype(jnp.float32), flat, by_lane, precision=highest
    )
    right_strip = lax.dot_general(
        (lanes == tile_cols - SWEEPS + picks).astype(jnp.float32), flat, by_lane, precision=highest
    )
    ends = tile_count - 1
    from_left = lax.ppermute(right_strip, "gy", [(i, i + 1) for i in range(ends)])
    from_right = lax.ppermute(left_strip, "gy", [(i + 1, i) for i in range(ends)])
    width = tile_cols + 2 * SWEEPS
    out_lanes = jnp.arange(width, dtype=jnp.int32)[None, :]
    side = jnp.dot(
        jnp.concatenate([from_left, from_right], axis=0).T,
        jnp.concatenate(
            [out_lanes == picks, out_lanes == tile_cols + SWEEPS + picks], axis=0
        ).astype(jnp.float32),
        precision=highest,
    )
    side = with_layout_constraint(side, Layout((0, 1)))
    middle = jnp.pad(flat, ((0, 0), (SWEEPS, SWEEPS)))
    both = (middle + side).reshape(stacked.shape[0], tiled_rows, width)[:, :halo_rows, :]
    field = both[:layers]
    padded_cond = both[layers:]
    row_at = (
        lax.axis_index("gx") * tile_rows - SWEEPS + jnp.arange(tile_rows + 2 * SWEEPS)
    )[:, None]
    col_at = (
        lax.axis_index("gy") * tile_cols - SWEEPS + jnp.arange(tile_cols + 2 * SWEEPS)
    )[None, :]
    inside = (
        (row_at >= 0)
        & (row_at < tile_rows * lax.axis_size("gx"))
        & (col_at >= 0)
        & (col_at < tile_cols * tile_count)
    )
    sides = conductances(padded_cond)
    for sweep_k in range(SWEEPS):
        window = [
            side[:, sweep_k : side.shape[1] - sweep_k, sweep_k : side.shape[2] - sweep_k]
            for side in sides
        ]
        field = lateral_core(field, window)
        if sweep_k < SWEEPS - 1:
            edge = sweep_k + 1
            field = jnp.where(inside[None, edge:-edge, edge:-edge], field, 0.0)
    surface = field[0]
    answered = jnp.dot(landing.T, surface, precision=highest).reshape(
        tile_count, capacity, tile_cols
    )
    returned = lax.all_to_all(answered, "gy", split_axis=0, concat_axis=0, tiled=True)
    saturation = jnp.einsum("tcb,tcj->bj", placing, returned, precision=highest)
    new_bottom = bottom + capillary * (saturation - in_use_f[:, None] * bottom)
    moisture_out = jnp.transpose(jnp.concatenate([wet[: depth - 1], new_bottom[None]]), (1, 0, 2))
    patch_hot = (patch_ids[None, :] == jnp.arange(PATCH_DEV, dtype=jnp.int32)[:, None]).astype(
        jnp.float32
    )
    patch_sums = jnp.dot(patch_hot, saturation, precision=highest)
    return (field, moisture_out, patch_sums)


def solution(mesh):
    placed = (
        P(("gx", "gy"), None, None),
        P(("gx", "gy"), None, None),
        P(("gx", "gy"), None),
        P(None, "gx", "gy"),
        P(None, "gx", "gy"),
        P(("gx", "gy")),
        P(("gx", "gy")),
        P(("gx", "gy")),
        P(("gx", "gy")),
    )
    return jax.shard_map(
        local,
        mesh=mesh,
        in_specs=placed,
        out_specs=(P(None, "gx", "gy"), P(("gx", "gy"), None, None), P(("gx", "gy"), None)),
        check_vma=False,
    )
```

```python
import jax
import jax.numpy as jnp
from jax import lax
from jax.sharding import PartitionSpec as P
from jax.experimental import pallas as pl
from jax.experimental.pallas import tpu as pltpu
from jax.experimental.layout import Layout, with_layout_constraint

PATCH_DEV = 8
SWEEPS = 6


flow_rate = 0.15
capillary = 0.5


def with_halo(cells, sides, width):
    for axis, dim in sides:
        count = lax.axis_size(axis)
        ends = count - 1
        head = lax.slice_in_dim(cells, 0, width, axis=dim)
        tail = lax.slice_in_dim(cells, cells.shape[dim] - width, cells.shape[dim], axis=dim)
        cells = jnp.concatenate(
            [
                lax.ppermute(tail, axis, [(i, (i + 1) % count) for i in range(ends)]),
                cells,
                lax.ppermute(head, axis, [((i + 1) % count, i) for i in range(ends)]),
            ],
            axis=dim,
        )
    return cells


def column_kernel(moist_ref, diff_ref, rain_ref, wet_ref, ratio_ref):
    depth = moist_ref.shape[0]

    def body(g, carry):
        rows = pl.ds(0, moist_ref.shape[1])
        ratio = None
        carried = None
        for layer_k in range(depth):
            lower_coef = diff_ref[layer_k, rows, :]
            source = moist_ref[layer_k, rows, :]
            if layer_k == 0:
                source = source + rain_ref[rows, :]
                pivot = 1.0 + lower_coef
                carried = source / pivot
            else:
                upper_coef = diff_ref[layer_k - 1, rows, :]
                pivot = 1.0 + lower_coef + upper_coef - upper_coef * ratio
                carried = (source + upper_coef * carried) / pivot
            ratio = lower_coef / pivot
            ratio_ref[layer_k, rows, :] = ratio
            wet_ref[layer_k, rows, :] = carried
        solved = carried
        for layer_k in range(depth - 2, -1, -1):
            solved = wet_ref[layer_k, rows, :] + ratio_ref[layer_k, rows, :] * solved
            wet_ref[layer_k, rows, :] = solved
        return carry

    body(0, 0)


def column_solve(moisture, diffusivity, rain):
    blocks, depth, lanes = moisture.shape
    layered = (depth, blocks, lanes)
    return pl.pallas_call(
        column_kernel,
        out_shape=jax.ShapeDtypeStruct(layered, jnp.float32),
        in_specs=[pl.BlockSpec(memory_space=pltpu.VMEM)] * 3,
        out_specs=pl.BlockSpec(memory_space=pltpu.VMEM),
        scratch_shapes=[pltpu.VMEM(layered, jnp.float32)],
        cost_estimate=pl.CostEstimate(
            flops=12 * blocks * depth * lanes, transcendentals=0, bytes_accessed=12 * blocks * depth * lanes
        ),
    )(jnp.transpose(moisture, (1, 0, 2)), jnp.transpose(diffusivity, (1, 0, 2)), rain)


SHIFTS = ((0, 1), (2, 1), (1, 0), (1, 2))


def conductances(padded_cond):
    inner_rows = padded_cond.shape[1] - 2
    inner_cols = padded_cond.shape[2] - 2
    centre_cond = padded_cond[:, 1:-1, 1:-1]
    sides = []
    for row_shift, col_shift in SHIFTS:
        beside_cond = padded_cond[
            :, row_shift : row_shift + inner_rows, col_shift : col_shift + inner_cols
        ]
        sides.append(0.5 * (centre_cond + beside_cond))
    sides.append(0.5 * (centre_cond[1:] + centre_cond[:-1]))
    return sides


def lateral_core(padded_head, sides):
    inner_rows = padded_head.shape[1] - 2
    inner_cols = padded_head.shape[2] - 2
    centre = padded_head[:, 1:-1, 1:-1]
    flux_total = jnp.zeros_like(centre)
    for (row_shift, col_shift), side in zip(SHIFTS, sides):
        beside = padded_head[
            :, row_shift : row_shift + inner_rows, col_shift : col_shift + inner_cols
        ]
        flux_total = flux_total + side * (beside - centre)
    vertical = sides[4] * (centre[1:] - centre[:-1])
    flux_total = (
        flux_total
        + jnp.pad(vertical, ((0, 1), (0, 0), (0, 0)))
        - jnp.pad(vertical, ((1, 0), (0, 0), (0, 0)))
    )
    return centre + flow_rate * flux_total


def local(moisture, diffusivity, rain, head, conductivity, tile_ids, offsets, patch_ids, counts):
    highest = lax.Precision.HIGHEST
    block_count = moisture.shape[0]
    tile_count = lax.axis_size("gy")
    capacity = block_count // 2
    tile_rows = head.shape[1]
    tile_cols = head.shape[2]
    wet = column_solve(moisture, diffusivity, rain)
    depth = moisture.shape[1]
    bottom = wet[depth - 1]
    drain = diffusivity[:, -1, :] * bottom
    in_use = jnp.arange(block_count, dtype=jnp.int32) < counts[0]
    in_use_f = in_use.astype(jnp.float32)
    to_tile = (
        (tile_ids[:, None] == jnp.arange(tile_count, dtype=jnp.int32)[None, :]) & in_use[:, None]
    ).astype(jnp.int32)
    earlier = (
        jnp.arange(block_count, dtype=jnp.int32)[None, :]
        < jnp.arange(block_count, dtype=jnp.int32)[:, None]
    ).astype(jnp.float32)
    before = jnp.dot(earlier, to_tile.astype(jnp.float32), precision=highest).astype(jnp.int32)
    slot_of = jnp.sum(before * to_tile, axis=1)
    slot_match = slot_of[None, None, :] == jnp.arange(capacity, dtype=jnp.int32)[None, :, None]
    placing = (to_tile.T[:, None, :] * slot_match).astype(jnp.float32)
    outgoing = jnp.einsum("tcb,bj->tcj", placing, drain, precision=highest)
    out_rows = (
        jnp.einsum("tcb,b->tc", placing, (offsets + 1).astype(jnp.float32), precision=highest) - 1.0
    )
    packed = jnp.concatenate(
        [outgoing, jnp.pad(out_rows, ((0, 0), (0, tile_cols - capacity)))[:, None, :]], axis=1
    )
    arrived = lax.all_to_all(packed, "gy", split_axis=0, concat_axis=0, tiled=True)
    incoming = arrived[:, :capacity, :]
    in_rows = arrived[:, capacity, :capacity]
    slot_total = tile_count * capacity
    landing = (
        in_rows.reshape(1, slot_total) == jnp.arange(tile_rows, dtype=jnp.float32)[:, None]
    ).astype(jnp.float32)
    recharge = jnp.dot(landing, incoming.reshape(slot_total, tile_cols), precision=highest)
    field = head.at[0].add(recharge)
    layers = field.shape[0]
    stacked = jnp.concatenate([field, conductivity], axis=0)
    rowed = with_halo(stacked, (("gx", 1),), SWEEPS)
    halo_rows = rowed.shape[1]
    tiled_rows = -(-halo_rows // 8) * 8
    flat = jnp.pad(rowed, ((0, 0), (0, tiled_rows - halo_rows), (0, 0))).reshape(-1, tile_cols)
    picks = jnp.arange(SWEEPS, dtype=jnp.int32)[:, None]
    lanes = jnp.arange(tile_cols, dtype=jnp.int32)[None, :]
    by_lane = (((1,), (1,)), ((), ()))
    left_strip = lax.dot_general(
        (lanes == picks).astype(jnp.float32), flat, by_lane, precision=highest
    )
    right_strip = lax.dot_general(
        (lanes == tile_cols - SWEEPS + picks).astype(jnp.float32), flat, by_lane, precision=highest
    )
    ends = tile_count - 1
    from_left = lax.ppermute(right_strip, "gy", [(i, i + 1) for i in range(ends)])
    from_right = lax.ppermute(left_strip, "gy", [(i + 1, i) for i in range(ends)])
    width = tile_cols + 2 * SWEEPS
    out_lanes = jnp.arange(width, dtype=jnp.int32)[None, :]
    side = jnp.dot(
        jnp.concatenate([from_left, from_right], axis=0).T,
        jnp.concatenate(
            [out_lanes == picks, out_lanes == tile_cols + SWEEPS + picks], axis=0
        ).astype(jnp.float32),
        precision=highest,
    )
    side = with_layout_constraint(side, Layout((0, 1)))
    middle = jnp.pad(flat, ((0, 0), (SWEEPS, SWEEPS)))
    both = (middle + side).reshape(stacked.shape[0], tiled_rows, width)[:, :halo_rows, :]
    field = both[:layers]
    padded_cond = both[layers:]
    row_at = (
        lax.axis_index("gx") * tile_rows - SWEEPS + jnp.arange(tile_rows + 2 * SWEEPS)
    )[:, None]
    col_at = (
        lax.axis_index("gy") * tile_cols - SWEEPS + jnp.arange(tile_cols + 2 * SWEEPS)
    )[None, :]
    inside = (
        (row_at >= 0)
        & (row_at < tile_rows * lax.axis_size("gx"))
        & (col_at >= 0)
        & (col_at < tile_cols * tile_count)
    )
    sides = conductances(padded_cond)
    for sweep_k in range(SWEEPS):
        window = [
            side[:, sweep_k : side.shape[1] - sweep_k, sweep_k : side.shape[2] - sweep_k]
            for side in sides
        ]
        field = lateral_core(field, window)
        if sweep_k < SWEEPS - 1:
            edge = sweep_k + 1
            field = jnp.where(inside[None, edge:-edge, edge:-edge], field, 0.0)
    surface = field[0]
    answered = jnp.dot(landing.T, surface, precision=highest).reshape(
        tile_count, capacity, tile_cols
    )
    returned = lax.all_to_all(answered, "gy", split_axis=0, concat_axis=0, tiled=True)
    saturation = jnp.einsum("tcb,tcj->bj", placing, returned, precision=highest)
    new_bottom = bottom + capillary * (saturation - in_use_f[:, None] * bottom)
    moisture_out = jnp.transpose(wet.at[depth - 1].set(new_bottom), (1, 0, 2))
    patch_hot = (patch_ids[None, :] == jnp.arange(PATCH_DEV, dtype=jnp.int32)[:, None]).astype(
        jnp.float32
    )
    patch_sums = jnp.dot(patch_hot, saturation, precision=highest)
    return (field, moisture_out, patch_sums)


def solution(mesh):
    placed = (
        P(("gx", "gy"), None, None),
        P(("gx", "gy"), None, None),
        P(("gx", "gy"), None),
        P(None, "gx", "gy"),
        P(None, "gx", "gy"),
        P(("gx", "gy")),
        P(("gx", "gy")),
        P(("gx", "gy")),
        P(("gx", "gy")),
    )
    return jax.shard_map(
        local,
        mesh=mesh,
        in_specs=placed,
        out_specs=(P(None, "gx", "gy"), P(("gx", "gy"), None, None), P(("gx", "gy"), None)),
        check_vma=False,
    )
```

```python
import jax
import jax.numpy as jnp
from jax import lax
from jax.sharding import PartitionSpec as P
from jax.experimental import pallas as pl
from jax.experimental.pallas import tpu as pltpu
from jax.experimental.layout import Layout, with_layout_constraint

PATCH_DEV = 8
SWEEPS = 6


flow_rate = 0.15
capillary = 0.5


def with_halo(cells, sides, width):
    for axis, dim in sides:
        count = lax.axis_size(axis)
        ends = count - 1
        head = lax.slice_in_dim(cells, 0, width, axis=dim)
        tail = lax.slice_in_dim(cells, cells.shape[dim] - width, cells.shape[dim], axis=dim)
        cells = jnp.concatenate(
            [
                lax.ppermute(tail, axis, [(i, (i + 1) % count) for i in range(ends)]),
                cells,
                lax.ppermute(head, axis, [((i + 1) % count, i) for i in range(ends)]),
            ],
            axis=dim,
        )
    return cells


def column_kernel(moist_ref, diff_ref, rain_ref, wet_ref, ratio_ref):
    depth = moist_ref.shape[0]

    def body(g, carry):
        rows = pl.ds(0, moist_ref.shape[1])
        ratio = None
        carried = None
        for layer_k in range(depth):
            lower_coef = diff_ref[layer_k, rows, :]
            source = moist_ref[layer_k, rows, :]
            if layer_k == 0:
                source = source + rain_ref[rows, :]
                pivot = 1.0 + lower_coef
                carried = source / pivot
            else:
                upper_coef = diff_ref[layer_k - 1, rows, :]
                pivot = 1.0 + lower_coef + upper_coef - upper_coef * ratio
                carried = (source + upper_coef * carried) / pivot
            ratio = lower_coef / pivot
            ratio_ref[layer_k, rows, :] = ratio
            wet_ref[layer_k, rows, :] = carried
        solved = carried
        for layer_k in range(depth - 2, -1, -1):
            solved = wet_ref[layer_k, rows, :] + ratio_ref[layer_k, rows, :] * solved
            wet_ref[layer_k, rows, :] = solved
        return carry

    body(0, 0)


def column_solve(moisture, diffusivity, rain):
    blocks, depth, lanes = moisture.shape
    layered = (depth, blocks, lanes)
    return pl.pallas_call(
        column_kernel,
        out_shape=jax.ShapeDtypeStruct(layered, jnp.float32),
        in_specs=[pl.BlockSpec(memory_space=pltpu.VMEM)] * 3,
        out_specs=pl.BlockSpec(memory_space=pltpu.VMEM),
        scratch_shapes=[pltpu.VMEM(layered, jnp.float32)],
        cost_estimate=pl.CostEstimate(
            flops=12 * blocks * depth * lanes, transcendentals=0, bytes_accessed=12 * blocks * depth * lanes
        ),
    )(jnp.transpose(moisture, (1, 0, 2)), jnp.transpose(diffusivity, (1, 0, 2)), rain)


SHIFTS = ((0, 1), (2, 1), (1, 0), (1, 2))


def conductances(padded_cond):
    inner_rows = padded_cond.shape[1] - 2
    inner_cols = padded_cond.shape[2] - 2
    centre_cond = padded_cond[:, 1:-1, 1:-1]
    sides = []
    for row_shift, col_shift in SHIFTS:
        beside_cond = padded_cond[
            :, row_shift : row_shift + inner_rows, col_shift : col_shift + inner_cols
        ]
        sides.append(0.5 * (centre_cond + beside_cond))
    sides.append(0.5 * (centre_cond[1:] + centre_cond[:-1]))
    return sides


def lateral_core(padded_head, sides):
    inner_rows = padded_head.shape[1] - 2
    inner_cols = padded_head.shape[2] - 2
    centre = padded_head[:, 1:-1, 1:-1]
    flux_total = jnp.zeros_like(centre)
    for (row_shift, col_shift), side in zip(SHIFTS, sides):
        beside = padded_head[
            :, row_shift : row_shift + inner_rows, col_shift : col_shift + inner_cols
        ]
        flux_total = flux_total + side * (beside - centre)
    vertical = sides[4] * (centre[1:] - centre[:-1])
    flux_total = (
        flux_total
        + jnp.pad(vertical, ((0, 1), (0, 0), (0, 0)))
        - jnp.pad(vertical, ((1, 0), (0, 0), (0, 0)))
    )
    return centre + flow_rate * flux_total


def local(moisture, diffusivity, rain, head, conductivity, tile_ids, offsets, patch_ids, counts):
    highest = lax.Precision.HIGHEST
    block_count = moisture.shape[0]
    tile_count = lax.axis_size("gy")
    capacity = block_count // 2
    tile_rows = head.shape[1]
    tile_cols = head.shape[2]
    wet = column_solve(moisture, diffusivity, rain)
    depth = moisture.shape[1]
    bottom = wet[depth - 1]
    drain = diffusivity[:, -1, :] * bottom
    in_use = jnp.arange(block_count, dtype=jnp.int32) < counts[0]
    in_use_f = in_use.astype(jnp.float32)
    to_tile = (
        (tile_ids[:, None] == jnp.arange(tile_count, dtype=jnp.int32)[None, :]) & in_use[:, None]
    ).astype(jnp.int32)
    earlier = (
        jnp.arange(block_count, dtype=jnp.int32)[None, :]
        < jnp.arange(block_count, dtype=jnp.int32)[:, None]
    ).astype(jnp.float32)
    before = jnp.dot(earlier, to_tile.astype(jnp.float32), precision=highest).astype(jnp.int32)
    slot_of = jnp.sum(before * to_tile, axis=1)
    slot_match = slot_of[None, None, :] == jnp.arange(capacity, dtype=jnp.int32)[None, :, None]
    placing = (to_tile.T[:, None, :] * slot_match).astype(jnp.float32)
    outgoing = jnp.einsum("tcb,bj->tcj", placing, drain, precision=highest)
    out_rows = (
        jnp.einsum("tcb,b->tc", placing, (offsets + 1).astype(jnp.float32), precision=highest) - 1.0
    )
    packed = jnp.concatenate(
        [outgoing, jnp.pad(out_rows, ((0, 0), (0, tile_cols - capacity)))[:, None, :]], axis=1
    )
    arrived = lax.all_to_all(packed, "gy", split_axis=0, concat_axis=0, tiled=True)
    incoming = arrived[:, :capacity, :]
    in_rows = arrived[:, capacity, :capacity]
    slot_total = tile_count * capacity
    landing = (
        in_rows.reshape(1, slot_total) == jnp.arange(tile_rows, dtype=jnp.float32)[:, None]
    ).astype(jnp.float32)
    recharge = jnp.dot(landing, incoming.reshape(slot_total, tile_cols), precision=highest)
    field = head.at[0].add(recharge)
    layers = field.shape[0]
    stacked = jnp.concatenate([field, conductivity], axis=0)
    rowed = with_halo(stacked, (("gx", 1),), SWEEPS)
    halo_rows = rowed.shape[1]
    tiled_rows = -(-halo_rows // 8) * 8
    flat = jnp.pad(rowed, ((0, 0), (0, tiled_rows - halo_rows), (0, 0))).reshape(-1, tile_cols)
    picks = jnp.arange(SWEEPS, dtype=jnp.int32)[:, None]
    lanes = jnp.arange(tile_cols, dtype=jnp.int32)[None, :]
    by_lane = (((1,), (1,)), ((), ()))
    spare = jnp.zeros((8 - SWEEPS % 8) % 8, jnp.int32)[:, None] - 1
    choose = jnp.concatenate(
        [lanes == jnp.concatenate([picks, spare]), lanes == tile_cols - SWEEPS + picks], axis=0
    ).astype(jnp.float32)
    strips = lax.dot_general(choose, flat, by_lane, precision=highest)
    gap = SWEEPS + spare.shape[0]
    left_strip = strips[:SWEEPS]
    right_strip = strips[gap : gap + SWEEPS]
    ends = tile_count - 1
    from_left = lax.ppermute(right_strip, "gy", [(i, i + 1) for i in range(ends)])
    from_right = lax.ppermute(left_strip, "gy", [(i + 1, i) for i in range(ends)])
    width = tile_cols + 2 * SWEEPS
    out_lanes = jnp.arange(width, dtype=jnp.int32)[None, :]
    side = jnp.dot(
        jnp.concatenate([from_left, from_right], axis=0).T,
        jnp.concatenate(
            [out_lanes == picks, out_lanes == tile_cols + SWEEPS + picks], axis=0
        ).astype(jnp.float32),
        precision=highest,
    )
    side = with_layout_constraint(side, Layout((0, 1)))
    middle = jnp.pad(flat, ((0, 0), (SWEEPS, SWEEPS)))
    both = (middle + side).reshape(stacked.shape[0], tiled_rows, width)[:, :halo_rows, :]
    field = both[:layers]
    padded_cond = both[layers:]
    row_at = (
        lax.axis_index("gx") * tile_rows - SWEEPS + jnp.arange(tile_rows + 2 * SWEEPS)
    )[:, None]
    col_at = (
        lax.axis_index("gy") * tile_cols - SWEEPS + jnp.arange(tile_cols + 2 * SWEEPS)
    )[None, :]
    inside = (
        (row_at >= 0)
        & (row_at < tile_rows * lax.axis_size("gx"))
        & (col_at >= 0)
        & (col_at < tile_cols * tile_count)
    )
    sides = conductances(padded_cond)
    for sweep_k in range(SWEEPS):
        window = [
            side[:, sweep_k : side.shape[1] - sweep_k, sweep_k : side.shape[2] - sweep_k]
            for side in sides
        ]
        field = lateral_core(field, window)
        if sweep_k < SWEEPS - 1:
            edge = sweep_k + 1
            field = jnp.where(inside[None, edge:-edge, edge:-edge], field, 0.0)
    surface = field[0]
    answered = jnp.dot(landing.T, surface, precision=highest).reshape(
        tile_count, capacity, tile_cols
    )
    returned = lax.all_to_all(answered, "gy", split_axis=0, concat_axis=0, tiled=True)
    saturation = jnp.einsum("tcb,tcj->bj", placing, returned, precision=highest)
    new_bottom = bottom + capillary * (saturation - in_use_f[:, None] * bottom)
    moisture_out = jnp.transpose(wet.at[depth - 1].set(new_bottom), (1, 0, 2))
    patch_hot = (patch_ids[None, :] == jnp.arange(PATCH_DEV, dtype=jnp.int32)[:, None]).astype(
        jnp.float32
    )
    patch_sums = jnp.dot(patch_hot, saturation, precision=highest)
    return (field, moisture_out, patch_sums)


def solution(mesh):
    placed = (
        P(("gx", "gy"), None, None),
        P(("gx", "gy"), None, None),
        P(("gx", "gy"), None),
        P(None, "gx", "gy"),
        P(None, "gx", "gy"),
        P(("gx", "gy")),
        P(("gx", "gy")),
        P(("gx", "gy")),
        P(("gx", "gy")),
    )
    return jax.shard_map(
        local,
        mesh=mesh,
        in_specs=placed,
        out_specs=(P(None, "gx", "gy"), P(("gx", "gy"), None, None), P(("gx", "gy"), None)),
        check_vma=False,
    )
```

```python
import jax
import jax.numpy as jnp
from jax import lax
from jax.sharding import PartitionSpec as P
from jax.experimental import pallas as pl
from jax.experimental.pallas import tpu as pltpu
from jax.experimental.layout import Layout, with_layout_constraint

PATCH_DEV = 8
SWEEPS = 6


flow_rate = 0.15
capillary = 0.5


def with_halo(cells, sides, width):
    for axis, dim in sides:
        count = lax.axis_size(axis)
        ends = count - 1
        head = lax.slice_in_dim(cells, 0, width, axis=dim)
        tail = lax.slice_in_dim(cells, cells.shape[dim] - width, cells.shape[dim], axis=dim)
        cells = jnp.concatenate(
            [
                lax.ppermute(tail, axis, [(i, (i + 1) % count) for i in range(ends)]),
                cells,
                lax.ppermute(head, axis, [((i + 1) % count, i) for i in range(ends)]),
            ],
            axis=dim,
        )
    return cells


def column_kernel(moist_ref, diff_ref, rain_ref, wet_ref, ratio_ref):
    depth = moist_ref.shape[0]

    def body(g, carry):
        rows = pl.ds(0, moist_ref.shape[1])
        ratio = None
        carried = None
        for layer_k in range(depth):
            lower_coef = diff_ref[layer_k, rows, :]
            source = moist_ref[layer_k, rows, :]
            if layer_k == 0:
                source = source + rain_ref[rows, :]
                pivot = 1.0 + lower_coef
                carried = source / pivot
            else:
                upper_coef = diff_ref[layer_k - 1, rows, :]
                pivot = 1.0 + lower_coef + upper_coef - upper_coef * ratio
                carried = (source + upper_coef * carried) / pivot
            ratio = lower_coef / pivot
            ratio_ref[layer_k, rows, :] = ratio
            wet_ref[layer_k, rows, :] = carried
        solved = carried
        for layer_k in range(depth - 2, -1, -1):
            solved = wet_ref[layer_k, rows, :] + ratio_ref[layer_k, rows, :] * solved
            wet_ref[layer_k, rows, :] = solved
        return carry

    body(0, 0)


def column_solve(moisture, diffusivity, rain):
    blocks, depth, lanes = moisture.shape
    layered = (depth, blocks, lanes)
    return pl.pallas_call(
        column_kernel,
        out_shape=jax.ShapeDtypeStruct(layered, jnp.float32),
        in_specs=[pl.BlockSpec(memory_space=pltpu.VMEM)] * 3,
        out_specs=pl.BlockSpec(memory_space=pltpu.VMEM),
        scratch_shapes=[pltpu.VMEM(layered, jnp.float32)],
        cost_estimate=pl.CostEstimate(
            flops=12 * blocks * depth * lanes, transcendentals=0, bytes_accessed=12 * blocks * depth * lanes
        ),
    )(jnp.transpose(moisture, (1, 0, 2)), jnp.transpose(diffusivity, (1, 0, 2)), rain)


SHIFTS = ((0, 1), (2, 1), (1, 0), (1, 2))


def conductances(padded_cond):
    inner_rows = padded_cond.shape[1] - 2
    inner_cols = padded_cond.shape[2] - 2
    centre_cond = padded_cond[:, 1:-1, 1:-1]
    sides = []
    for row_shift, col_shift in SHIFTS:
        beside_cond = padded_cond[
            :, row_shift : row_shift + inner_rows, col_shift : col_shift + inner_cols
        ]
        sides.append(0.5 * (centre_cond + beside_cond))
    sides.append(0.5 * (centre_cond[1:] + centre_cond[:-1]))
    return sides


def lateral_core(padded_head, sides):
    inner_rows = padded_head.shape[1] - 2
    inner_cols = padded_head.shape[2] - 2
    centre = padded_head[:, 1:-1, 1:-1]
    flux_total = jnp.zeros_like(centre)
    for (row_shift, col_shift), side in zip(SHIFTS, sides):
        beside = padded_head[
            :, row_shift : row_shift + inner_rows, col_shift : col_shift + inner_cols
        ]
        flux_total = flux_total + side * (beside - centre)
    vertical = sides[4] * (centre[1:] - centre[:-1])
    flux_total = (
        flux_total
        + jnp.pad(vertical, ((0, 1), (0, 0), (0, 0)))
        - jnp.pad(vertical, ((1, 0), (0, 0), (0, 0)))
    )
    return centre + flow_rate * flux_total


def local(moisture, diffusivity, rain, head, conductivity, tile_ids, offsets, patch_ids, counts):
    highest = lax.Precision.HIGHEST
    block_count = moisture.shape[0]
    tile_count = lax.axis_size("gy")
    tile_rows = head.shape[1]
    tile_cols = head.shape[2]
    wet = column_solve(moisture, diffusivity, rain)
    depth = moisture.shape[1]
    bottom = wet[depth - 1]
    drain = diffusivity[:, -1, :] * bottom
    in_use = jnp.arange(block_count, dtype=jnp.int32) < counts[0]
    in_use_f = in_use.astype(jnp.float32)
    tiles = jnp.arange(tile_count, dtype=jnp.int32)
    sent = (tile_ids[None, :] == tiles[:, None]) & in_use[None, :]
    outgoing = jnp.where(sent[:, :, None], drain[None], 0.0)
    out_rows = jnp.where(sent, offsets[None, :].astype(jnp.float32), -1.0)
    packed = jnp.concatenate(
        [outgoing, jnp.pad(out_rows, ((0, 0), (0, tile_cols - block_count)), constant_values=-1.0)[:, None, :]],
        axis=1,
    )
    arrived = lax.all_to_all(packed, "gy", split_axis=0, concat_axis=0, tiled=True)
    incoming = arrived[:, :block_count, :]
    in_rows = arrived[:, block_count, :block_count]
    slot_total = tile_count * block_count
    landing = (
        in_rows.reshape(1, slot_total) == jnp.arange(tile_rows, dtype=jnp.float32)[:, None]
    ).astype(jnp.float32)
    recharge = jnp.dot(landing, incoming.reshape(slot_total, tile_cols), precision=highest)
    field = head.at[0].add(recharge)
    layers = field.shape[0]
    stacked = jnp.concatenate([field, conductivity], axis=0)
    rowed = with_halo(stacked, (("gx", 1),), SWEEPS)
    halo_rows = rowed.shape[1]
    tiled_rows = -(-halo_rows // 8) * 8
    flat = jnp.pad(rowed, ((0, 0), (0, tiled_rows - halo_rows), (0, 0))).reshape(-1, tile_cols)
    picks = jnp.arange(SWEEPS, dtype=jnp.int32)[:, None]
    lanes = jnp.arange(tile_cols, dtype=jnp.int32)[None, :]
    by_lane = (((1,), (1,)), ((), ()))
    spare = jnp.zeros((8 - SWEEPS % 8) % 8, jnp.int32)[:, None] - 1
    choose = jnp.concatenate(
        [lanes == jnp.concatenate([picks, spare]), lanes == tile_cols - SWEEPS + picks], axis=0
    ).astype(jnp.float32)
    strips = lax.dot_general(choose, flat, by_lane, precision=highest)
    gap = SWEEPS + spare.shape[0]
    left_strip = strips[:SWEEPS]
    right_strip = strips[gap : gap + SWEEPS]
    ends = tile_count - 1
    from_left = lax.ppermute(right_strip, "gy", [(i, i + 1) for i in range(ends)])
    from_right = lax.ppermute(left_strip, "gy", [(i + 1, i) for i in range(ends)])
    width = tile_cols + 2 * SWEEPS
    out_lanes = jnp.arange(width, dtype=jnp.int32)[None, :]
    side = jnp.dot(
        jnp.concatenate([from_left, from_right], axis=0).T,
        jnp.concatenate(
            [out_lanes == picks, out_lanes == tile_cols + SWEEPS + picks], axis=0
        ).astype(jnp.float32),
        precision=highest,
    )
    side = with_layout_constraint(side, Layout((0, 1)))
    middle = jnp.pad(flat, ((0, 0), (SWEEPS, SWEEPS)))
    both = (middle + side).reshape(stacked.shape[0], tiled_rows, width)[:, :halo_rows, :]
    field = both[:layers]
    padded_cond = both[layers:]
    row_at = (
        lax.axis_index("gx") * tile_rows - SWEEPS + jnp.arange(tile_rows + 2 * SWEEPS)
    )[:, None]
    col_at = (
        lax.axis_index("gy") * tile_cols - SWEEPS + jnp.arange(tile_cols + 2 * SWEEPS)
    )[None, :]
    inside = (
        (row_at >= 0)
        & (row_at < tile_rows * lax.axis_size("gx"))
        & (col_at >= 0)
        & (col_at < tile_cols * tile_count)
    )
    sides = conductances(padded_cond)
    for sweep_k in range(SWEEPS):
        window = [
            side[:, sweep_k : side.shape[1] - sweep_k, sweep_k : side.shape[2] - sweep_k]
            for side in sides
        ]
        field = lateral_core(field, window)
        if sweep_k < SWEEPS - 1:
            edge = sweep_k + 1
            field = jnp.where(inside[None, edge:-edge, edge:-edge], field, 0.0)
    surface = field[0]
    answered = jnp.dot(landing.T, surface, precision=highest).reshape(
        tile_count, block_count, tile_cols
    )
    returned = lax.all_to_all(answered, "gy", split_axis=0, concat_axis=0, tiled=True)
    saturation = jnp.zeros_like(drain)
    for tile in range(tile_count):
        saturation = jnp.where(sent[tile][:, None], returned[tile], saturation)
    new_bottom = bottom + capillary * (saturation - in_use_f[:, None] * bottom)
    moisture_out = jnp.transpose(wet.at[depth - 1].set(new_bottom), (1, 0, 2))
    patch_hot = (patch_ids[None, :] == jnp.arange(PATCH_DEV, dtype=jnp.int32)[:, None]).astype(
        jnp.float32
    )
    patch_sums = jnp.dot(patch_hot, saturation, precision=highest)
    return (field, moisture_out, patch_sums)


def solution(mesh):
    placed = (
        P(("gx", "gy"), None, None),
        P(("gx", "gy"), None, None),
        P(("gx", "gy"), None),
        P(None, "gx", "gy"),
        P(None, "gx", "gy"),
        P(("gx", "gy")),
        P(("gx", "gy")),
        P(("gx", "gy")),
        P(("gx", "gy")),
    )
    return jax.shard_map(
        local,
        mesh=mesh,
        in_specs=placed,
        out_specs=(P(None, "gx", "gy"), P(("gx", "gy"), None, None), P(("gx", "gy"), None)),
        check_vma=False,
    )
```

```python
import jax
import jax.numpy as jnp
from jax import lax
from jax.sharding import PartitionSpec as P
from jax.experimental import pallas as pl
from jax.experimental.pallas import tpu as pltpu
from jax.experimental.layout import Layout, with_layout_constraint

PATCH_DEV = 8
SWEEPS = 6


flow_rate = 0.15
capillary = 0.5


def with_halo(cells, sides, width):
    for axis, dim in sides:
        count = lax.axis_size(axis)
        ends = count - 1
        head = lax.slice_in_dim(cells, 0, width, axis=dim)
        tail = lax.slice_in_dim(cells, cells.shape[dim] - width, cells.shape[dim], axis=dim)
        cells = jnp.concatenate(
            [
                lax.ppermute(tail, axis, [(i, (i + 1) % count) for i in range(ends)]),
                cells,
                lax.ppermute(head, axis, [((i + 1) % count, i) for i in range(ends)]),
            ],
            axis=dim,
        )
    return cells


def column_kernel(moist_ref, diff_ref, rain_ref, wet_ref, ratio_ref):
    depth = moist_ref.shape[0]

    def body(g, carry):
        rows = pl.ds(0, moist_ref.shape[1])
        ratio = None
        carried = None
        for layer_k in range(depth):
            lower_coef = diff_ref[layer_k, rows, :]
            source = moist_ref[layer_k, rows, :]
            if layer_k == 0:
                source = source + rain_ref[rows, :]
                pivot = 1.0 + lower_coef
                carried = source / pivot
            else:
                upper_coef = diff_ref[layer_k - 1, rows, :]
                pivot = 1.0 + lower_coef + upper_coef - upper_coef * ratio
                carried = (source + upper_coef * carried) / pivot
            ratio = lower_coef / pivot
            ratio_ref[layer_k, rows, :] = ratio
            wet_ref[layer_k, rows, :] = carried
        solved = carried
        for layer_k in range(depth - 2, -1, -1):
            solved = wet_ref[layer_k, rows, :] + ratio_ref[layer_k, rows, :] * solved
            wet_ref[layer_k, rows, :] = solved
        return carry

    body(0, 0)


def column_solve(moisture, diffusivity, rain):
    blocks, depth, lanes = moisture.shape
    layered = (depth, blocks, lanes)
    return pl.pallas_call(
        column_kernel,
        out_shape=jax.ShapeDtypeStruct(layered, jnp.float32),
        in_specs=[pl.BlockSpec(memory_space=pltpu.VMEM)] * 3,
        out_specs=pl.BlockSpec(memory_space=pltpu.VMEM),
        scratch_shapes=[pltpu.VMEM(layered, jnp.float32)],
        cost_estimate=pl.CostEstimate(
            flops=12 * blocks * depth * lanes, transcendentals=0, bytes_accessed=12 * blocks * depth * lanes
        ),
    )(jnp.transpose(moisture, (1, 0, 2)), jnp.transpose(diffusivity, (1, 0, 2)), rain)


SHIFTS = ((0, 1), (2, 1), (1, 0), (1, 2))


def conductances(padded_cond):
    inner_rows = padded_cond.shape[1] - 2
    inner_cols = padded_cond.shape[2] - 2
    centre_cond = padded_cond[:, 1:-1, 1:-1]
    sides = []
    for row_shift, col_shift in SHIFTS:
        beside_cond = padded_cond[
            :, row_shift : row_shift + inner_rows, col_shift : col_shift + inner_cols
        ]
        sides.append(0.5 * (centre_cond + beside_cond))
    sides.append(0.5 * (centre_cond[1:] + centre_cond[:-1]))
    return sides


def lateral_core(padded_head, sides):
    inner_rows = padded_head.shape[1] - 2
    inner_cols = padded_head.shape[2] - 2
    centre = padded_head[:, 1:-1, 1:-1]
    flux_total = jnp.zeros_like(centre)
    for (row_shift, col_shift), side in zip(SHIFTS, sides):
        beside = padded_head[
            :, row_shift : row_shift + inner_rows, col_shift : col_shift + inner_cols
        ]
        flux_total = flux_total + side * (beside - centre)
    vertical = sides[4] * (centre[1:] - centre[:-1])
    flux_total = (
        flux_total
        + jnp.pad(vertical, ((0, 1), (0, 0), (0, 0)))
        - jnp.pad(vertical, ((1, 0), (0, 0), (0, 0)))
    )
    return centre + flow_rate * flux_total


def local(moisture, diffusivity, rain, head, conductivity, tile_ids, offsets, patch_ids, counts):
    highest = lax.Precision.HIGHEST
    block_count = moisture.shape[0]
    tile_count = lax.axis_size("gy")
    capacity = block_count // 2
    tile_rows = head.shape[1]
    tile_cols = head.shape[2]
    wet = column_solve(moisture, diffusivity, rain)
    depth = moisture.shape[1]
    bottom = wet[depth - 1]
    drain = diffusivity[:, -1, :] * bottom
    in_use = jnp.arange(block_count, dtype=jnp.int32) < counts[0]
    in_use_f = in_use.astype(jnp.float32)
    to_tile = (
        (tile_ids[:, None] == jnp.arange(tile_count, dtype=jnp.int32)[None, :]) & in_use[:, None]
    ).astype(jnp.int32)
    earlier = (
        jnp.arange(block_count, dtype=jnp.int32)[None, :]
        < jnp.arange(block_count, dtype=jnp.int32)[:, None]
    ).astype(jnp.float32)
    before = jnp.dot(earlier, to_tile.astype(jnp.float32), precision=highest).astype(jnp.int32)
    slot_of = jnp.sum(before * to_tile, axis=1)
    slot_match = slot_of[None, None, :] == jnp.arange(capacity, dtype=jnp.int32)[None, :, None]
    placing = (to_tile.T[:, None, :] * slot_match).astype(jnp.float32)
    outgoing = jnp.einsum("tcb,bj->tcj", placing, drain, precision=highest)
    out_rows = (
        jnp.einsum("tcb,b->tc", placing, (offsets + 1).astype(jnp.float32), precision=highest) - 1.0
    )
    packed = jnp.concatenate(
        [outgoing, jnp.pad(out_rows, ((0, 0), (0, tile_cols - capacity)))[:, None, :]], axis=1
    )
    arrived = lax.all_to_all(packed, "gy", split_axis=0, concat_axis=0, tiled=True)
    incoming = arrived[:, :capacity, :]
    in_rows = arrived[:, capacity, :capacity]
    slot_total = tile_count * capacity
    landing = (
        in_rows.reshape(1, slot_total) == jnp.arange(tile_rows, dtype=jnp.float32)[:, None]
    ).astype(jnp.float32)
    recharge = jnp.dot(landing, incoming.reshape(slot_total, tile_cols), precision=highest)
    field = head.at[0].add(recharge)
    layers = field.shape[0]
    stacked = jnp.concatenate([field, conductivity], axis=0)
    rows_count = lax.axis_size("gx")
    rows_end = rows_count - 1
    dense = (stacked.shape[0] * SWEEPS, tile_cols)
    from_above = lax.ppermute(
        stacked[:, tile_rows - SWEEPS :, :].reshape(dense),
        "gx",
        [(i, i + 1) for i in range(rows_end)],
    )
    from_below = lax.ppermute(
        stacked[:, :SWEEPS, :].reshape(dense), "gx", [(i + 1, i) for i in range(rows_end)]
    )
    halo_shape = (stacked.shape[0], SWEEPS, tile_cols)
    rowed = jnp.concatenate(
        [from_above.reshape(halo_shape), stacked, from_below.reshape(halo_shape)], axis=1
    )
    halo_rows = rowed.shape[1]
    tiled_rows = -(-halo_rows // 8) * 8
    flat = jnp.pad(rowed, ((0, 0), (0, tiled_rows - halo_rows), (0, 0))).reshape(-1, tile_cols)
    picks = jnp.arange(SWEEPS, dtype=jnp.int32)[:, None]
    lanes = jnp.arange(tile_cols, dtype=jnp.int32)[None, :]
    by_lane = (((1,), (1,)), ((), ()))
    spare = jnp.zeros((8 - SWEEPS % 8) % 8, jnp.int32)[:, None] - 1
    choose = jnp.concatenate(
        [lanes == jnp.concatenate([picks, spare]), lanes == tile_cols - SWEEPS + picks], axis=0
    ).astype(jnp.float32)
    strips = lax.dot_general(choose, flat, by_lane, precision=highest)
    gap = SWEEPS + spare.shape[0]
    left_strip = strips[:SWEEPS]
    right_strip = strips[gap : gap + SWEEPS]
    ends = tile_count - 1
    from_left = lax.ppermute(right_strip, "gy", [(i, i + 1) for i in range(ends)])
    from_right = lax.ppermute(left_strip, "gy", [(i + 1, i) for i in range(ends)])
    width = tile_cols + 2 * SWEEPS
    out_lanes = jnp.arange(width, dtype=jnp.int32)[None, :]
    side = jnp.dot(
        jnp.concatenate([from_left, from_right], axis=0).T,
        jnp.concatenate(
            [out_lanes == picks, out_lanes == tile_cols + SWEEPS + picks], axis=0
        ).astype(jnp.float32),
        precision=highest,
    )
    side = with_layout_constraint(side, Layout((0, 1)))
    middle = jnp.pad(flat, ((0, 0), (SWEEPS, SWEEPS)))
    both = (middle + side).reshape(stacked.shape[0], tiled_rows, width)[:, :halo_rows, :]
    field = both[:layers]
    padded_cond = both[layers:]
    row_at = (
        lax.axis_index("gx") * tile_rows - SWEEPS + jnp.arange(tile_rows + 2 * SWEEPS)
    )[:, None]
    col_at = (
        lax.axis_index("gy") * tile_cols - SWEEPS + jnp.arange(tile_cols + 2 * SWEEPS)
    )[None, :]
    inside = (
        (row_at >= 0)
        & (row_at < tile_rows * lax.axis_size("gx"))
        & (col_at >= 0)
        & (col_at < tile_cols * tile_count)
    )
    sides = conductances(padded_cond)
    for sweep_k in range(SWEEPS):
        window = [
            side[:, sweep_k : side.shape[1] - sweep_k, sweep_k : side.shape[2] - sweep_k]
            for side in sides
        ]
        field = lateral_core(field, window)
        if sweep_k < SWEEPS - 1:
            edge = sweep_k + 1
            field = jnp.where(inside[None, edge:-edge, edge:-edge], field, 0.0)
    surface = field[0]
    answered = jnp.dot(landing.T, surface, precision=highest).reshape(
        tile_count, capacity, tile_cols
    )
    returned = lax.all_to_all(answered, "gy", split_axis=0, concat_axis=0, tiled=True)
    saturation = jnp.einsum("tcb,tcj->bj", placing, returned, precision=highest)
    new_bottom = bottom + capillary * (saturation - in_use_f[:, None] * bottom)
    moisture_out = jnp.transpose(wet.at[depth - 1].set(new_bottom), (1, 0, 2))
    patch_hot = (patch_ids[None, :] == jnp.arange(PATCH_DEV, dtype=jnp.int32)[:, None]).astype(
        jnp.float32
    )
    patch_sums = jnp.dot(patch_hot, saturation, precision=highest)
    return (field, moisture_out, patch_sums)


def solution(mesh):
    placed = (
        P(("gx", "gy"), None, None),
        P(("gx", "gy"), None, None),
        P(("gx", "gy"), None),
        P(None, "gx", "gy"),
        P(None, "gx", "gy"),
        P(("gx", "gy")),
        P(("gx", "gy")),
        P(("gx", "gy")),
        P(("gx", "gy")),
    )
    return jax.shard_map(
        local,
        mesh=mesh,
        in_specs=placed,
        out_specs=(P(None, "gx", "gy"), P(("gx", "gy"), None, None), P(("gx", "gy"), None)),
        check_vma=False,
    )
```

```python
import jax
import jax.numpy as jnp
from jax import lax
from jax.sharding import PartitionSpec as P
from jax.experimental import pallas as pl
from jax.experimental.pallas import tpu as pltpu
from jax.experimental.layout import Layout, with_layout_constraint

PATCH_DEV = 8
SWEEPS = 6


flow_rate = 0.15
capillary = 0.5


def with_halo(cells, sides, width):
    for axis, dim in sides:
        count = lax.axis_size(axis)
        ends = count - 1
        head = lax.slice_in_dim(cells, 0, width, axis=dim)
        tail = lax.slice_in_dim(cells, cells.shape[dim] - width, cells.shape[dim], axis=dim)
        cells = jnp.concatenate(
            [
                lax.ppermute(tail, axis, [(i, (i + 1) % count) for i in range(ends)]),
                cells,
                lax.ppermute(head, axis, [((i + 1) % count, i) for i in range(ends)]),
            ],
            axis=dim,
        )
    return cells


def column_kernel(moist_ref, diff_ref, rain_ref, wet_ref, ratio_ref):
    depth = moist_ref.shape[0]

    def body(g, carry):
        rows = pl.ds(0, moist_ref.shape[1])
        ratio = None
        carried = None
        for layer_k in range(depth):
            lower_coef = diff_ref[layer_k, rows, :]
            source = moist_ref[layer_k, rows, :]
            if layer_k == 0:
                source = source + rain_ref[rows, :]
                pivot = 1.0 + lower_coef
                carried = source / pivot
            else:
                upper_coef = diff_ref[layer_k - 1, rows, :]
                pivot = 1.0 + lower_coef + upper_coef - upper_coef * ratio
                carried = (source + upper_coef * carried) / pivot
            ratio = lower_coef / pivot
            ratio_ref[layer_k, rows, :] = ratio
            wet_ref[layer_k, rows, :] = carried
        solved = carried
        for layer_k in range(depth - 2, -1, -1):
            solved = wet_ref[layer_k, rows, :] + ratio_ref[layer_k, rows, :] * solved
            wet_ref[layer_k, rows, :] = solved
        return carry

    body(0, 0)


def column_solve(moisture, diffusivity, rain):
    blocks, depth, lanes = moisture.shape
    layered = (depth, blocks, lanes)
    return pl.pallas_call(
        column_kernel,
        out_shape=jax.ShapeDtypeStruct(layered, jnp.float32),
        in_specs=[pl.BlockSpec(memory_space=pltpu.VMEM)] * 3,
        out_specs=pl.BlockSpec(memory_space=pltpu.VMEM),
        scratch_shapes=[pltpu.VMEM(layered, jnp.float32)],
        cost_estimate=pl.CostEstimate(
            flops=12 * blocks * depth * lanes, transcendentals=0, bytes_accessed=12 * blocks * depth * lanes
        ),
    )(jnp.transpose(moisture, (1, 0, 2)), jnp.transpose(diffusivity, (1, 0, 2)), rain)


SHIFTS = ((0, 1), (2, 1), (1, 0), (1, 2))


def conductances(padded_cond):
    inner_rows = padded_cond.shape[1] - 2
    inner_cols = padded_cond.shape[2] - 2
    centre_cond = padded_cond[:, 1:-1, 1:-1]
    sides = []
    for row_shift, col_shift in SHIFTS:
        beside_cond = padded_cond[
            :, row_shift : row_shift + inner_rows, col_shift : col_shift + inner_cols
        ]
        sides.append(0.5 * (centre_cond + beside_cond))
    sides.append(0.5 * (centre_cond[1:] + centre_cond[:-1]))
    return sides


def lateral_core(padded_head, sides):
    inner_rows = padded_head.shape[1] - 2
    inner_cols = padded_head.shape[2] - 2
    centre = padded_head[:, 1:-1, 1:-1]
    flux_total = jnp.zeros_like(centre)
    for (row_shift, col_shift), side in zip(SHIFTS, sides):
        beside = padded_head[
            :, row_shift : row_shift + inner_rows, col_shift : col_shift + inner_cols
        ]
        flux_total = flux_total + side * (beside - centre)
    vertical = sides[4] * (centre[1:] - centre[:-1])
    flux_total = (
        flux_total
        + jnp.pad(vertical, ((0, 1), (0, 0), (0, 0)))
        - jnp.pad(vertical, ((1, 0), (0, 0), (0, 0)))
    )
    return centre + flow_rate * flux_total


def local(moisture, diffusivity, rain, head, conductivity, tile_ids, offsets, patch_ids, counts):
    highest = lax.Precision.HIGHEST
    block_count = moisture.shape[0]
    tile_count = lax.axis_size("gy")
    capacity = block_count // 2
    tile_rows = head.shape[1]
    tile_cols = head.shape[2]
    wet = column_solve(moisture, diffusivity, rain)
    depth = moisture.shape[1]
    bottom = wet[depth - 1]
    drain = diffusivity[:, -1, :] * bottom
    in_use = jnp.arange(block_count, dtype=jnp.int32) < counts[0]
    in_use_f = in_use.astype(jnp.float32)
    to_tile = (
        (tile_ids[:, None] == jnp.arange(tile_count, dtype=jnp.int32)[None, :]) & in_use[:, None]
    ).astype(jnp.int32)
    earlier = (
        jnp.arange(block_count, dtype=jnp.int32)[None, :]
        < jnp.arange(block_count, dtype=jnp.int32)[:, None]
    ).astype(jnp.float32)
    before = jnp.dot(earlier, to_tile.astype(jnp.float32), precision=highest).astype(jnp.int32)
    slot_of = jnp.sum(before * to_tile, axis=1)
    slot_match = slot_of[None, None, :] == jnp.arange(capacity, dtype=jnp.int32)[None, :, None]
    placing = (to_tile.T[:, None, :] * slot_match).astype(jnp.float32)
    outgoing = jnp.einsum("tcb,bj->tcj", placing, drain, precision=highest)
    out_rows = (
        jnp.einsum("tcb,b->tc", placing, (offsets + 1).astype(jnp.float32), precision=highest) - 1.0
    )
    packed = jnp.concatenate(
        [outgoing, jnp.pad(out_rows, ((0, 0), (0, tile_cols - capacity)))[:, None, :]], axis=1
    )
    arrived = lax.all_to_all(packed, "gy", split_axis=0, concat_axis=0, tiled=True)
    incoming = arrived[:, :capacity, :]
    in_rows = arrived[:, capacity, :capacity]
    slot_total = tile_count * capacity
    landing = (
        in_rows.reshape(1, slot_total) == jnp.arange(tile_rows, dtype=jnp.float32)[:, None]
    ).astype(jnp.float32)
    recharge = jnp.dot(landing, incoming.reshape(slot_total, tile_cols), precision=highest)
    field = head.at[0].add(recharge)
    layers = field.shape[0]
    stacked = jnp.concatenate([field, conductivity], axis=0)
    rows_count = lax.axis_size("gx")
    rows_end = rows_count - 1
    dense = (stacked.shape[0] * SWEEPS, tile_cols)
    from_above = lax.ppermute(
        stacked[:, tile_rows - SWEEPS :, :].reshape(dense),
        "gx",
        [(i, i + 1) for i in range(rows_end)],
    )
    from_below = lax.ppermute(
        stacked[:, :SWEEPS, :].reshape(dense), "gx", [(i + 1, i) for i in range(rows_end)]
    )
    halo_shape = (stacked.shape[0], SWEEPS, tile_cols)
    rowed = jnp.concatenate(
        [from_above.reshape(halo_shape), stacked, from_below.reshape(halo_shape)], axis=1
    )
    halo_rows = rowed.shape[1]
    tiled_rows = -(-halo_rows // 8) * 8
    flat = jnp.pad(rowed, ((0, 0), (0, tiled_rows - halo_rows), (0, 0))).reshape(-1, tile_cols)
    picks = jnp.arange(SWEEPS, dtype=jnp.int32)[:, None]
    lanes = jnp.arange(tile_cols, dtype=jnp.int32)[None, :]
    by_lane = (((1,), (1,)), ((), ()))
    spare = jnp.zeros((8 - SWEEPS % 8) % 8, jnp.int32)[:, None] - 1
    choose = jnp.concatenate(
        [lanes == jnp.concatenate([picks, spare]), lanes == tile_cols - SWEEPS + picks], axis=0
    ).astype(jnp.float32)
    strips = lax.dot_general(choose, flat, by_lane, precision=highest)
    gap = SWEEPS + spare.shape[0]
    left_strip = strips[:SWEEPS]
    right_strip = strips[gap : gap + SWEEPS]
    ends = tile_count - 1
    strip_shape = left_strip.shape
    packed_strip = (strip_shape[0] * strip_shape[1] // tile_cols, tile_cols)
    from_left = lax.ppermute(
        right_strip.reshape(packed_strip), "gy", [(i, i + 1) for i in range(ends)]
    ).reshape(strip_shape)
    from_right = lax.ppermute(
        left_strip.reshape(packed_strip), "gy", [(i + 1, i) for i in range(ends)]
    ).reshape(strip_shape)
    width = tile_cols + 2 * SWEEPS
    out_lanes = jnp.arange(width, dtype=jnp.int32)[None, :]
    side = jnp.dot(
        jnp.concatenate([from_left, from_right], axis=0).T,
        jnp.concatenate(
            [out_lanes == picks, out_lanes == tile_cols + SWEEPS + picks], axis=0
        ).astype(jnp.float32),
        precision=highest,
    )
    side = with_layout_constraint(side, Layout((0, 1)))
    middle = jnp.pad(flat, ((0, 0), (SWEEPS, SWEEPS)))
    both = (middle + side).reshape(stacked.shape[0], tiled_rows, width)[:, :halo_rows, :]
    field = both[:layers]
    padded_cond = both[layers:]
    row_at = (
        lax.axis_index("gx") * tile_rows - SWEEPS + jnp.arange(tile_rows + 2 * SWEEPS)
    )[:, None]
    col_at = (
        lax.axis_index("gy") * tile_cols - SWEEPS + jnp.arange(tile_cols + 2 * SWEEPS)
    )[None, :]
    inside = (
        (row_at >= 0)
        & (row_at < tile_rows * lax.axis_size("gx"))
        & (col_at >= 0)
        & (col_at < tile_cols * tile_count)
    )
    sides = conductances(padded_cond)
    for sweep_k in range(SWEEPS):
        window = [
            side[:, sweep_k : side.shape[1] - sweep_k, sweep_k : side.shape[2] - sweep_k]
            for side in sides
        ]
        field = lateral_core(field, window)
        if sweep_k < SWEEPS - 1:
            edge = sweep_k + 1
            field = jnp.where(inside[None, edge:-edge, edge:-edge], field, 0.0)
    surface = field[0]
    answered = jnp.dot(landing.T, surface, precision=highest).reshape(
        tile_count, capacity, tile_cols
    )
    returned = lax.all_to_all(answered, "gy", split_axis=0, concat_axis=0, tiled=True)
    saturation = jnp.einsum("tcb,tcj->bj", placing, returned, precision=highest)
    new_bottom = bottom + capillary * (saturation - in_use_f[:, None] * bottom)
    moisture_out = jnp.transpose(wet.at[depth - 1].set(new_bottom), (1, 0, 2))
    patch_hot = (patch_ids[None, :] == jnp.arange(PATCH_DEV, dtype=jnp.int32)[:, None]).astype(
        jnp.float32
    )
    patch_sums = jnp.dot(patch_hot, saturation, precision=highest)
    return (field, moisture_out, patch_sums)


def solution(mesh):
    placed = (
        P(("gx", "gy"), None, None),
        P(("gx", "gy"), None, None),
        P(("gx", "gy"), None),
        P(None, "gx", "gy"),
        P(None, "gx", "gy"),
        P(("gx", "gy")),
        P(("gx", "gy")),
        P(("gx", "gy")),
        P(("gx", "gy")),
    )
    return jax.shard_map(
        local,
        mesh=mesh,
        in_specs=placed,
        out_specs=(P(None, "gx", "gy"), P(("gx", "gy"), None, None), P(("gx", "gy"), None)),
        check_vma=False,
    )
```

```python
import jax
import jax.numpy as jnp
from jax import lax
from jax.sharding import PartitionSpec as P
from jax.experimental import pallas as pl
from jax.experimental.pallas import tpu as pltpu
from jax.experimental.layout import Layout, with_layout_constraint

PATCH_DEV = 8
SWEEPS = 6


flow_rate = 0.15
capillary = 0.5


def with_halo(cells, sides, width):
    for axis, dim in sides:
        count = lax.axis_size(axis)
        ends = count - 1
        head = lax.slice_in_dim(cells, 0, width, axis=dim)
        tail = lax.slice_in_dim(cells, cells.shape[dim] - width, cells.shape[dim], axis=dim)
        cells = jnp.concatenate(
            [
                lax.ppermute(tail, axis, [(i, (i + 1) % count) for i in range(ends)]),
                cells,
                lax.ppermute(head, axis, [((i + 1) % count, i) for i in range(ends)]),
            ],
            axis=dim,
        )
    return cells


def column_kernel(moist_ref, diff_ref, rain_ref, wet_ref, drain_ref, ratio_ref):
    depth = moist_ref.shape[0]

    def body(g, carry):
        rows = pl.ds(0, moist_ref.shape[1])
        ratio = None
        carried = None
        for layer_k in range(depth):
            lower_coef = diff_ref[layer_k, rows, :]
            source = moist_ref[layer_k, rows, :]
            if layer_k == 0:
                source = source + rain_ref[rows, :]
                pivot = 1.0 + lower_coef
                carried = source / pivot
            else:
                upper_coef = diff_ref[layer_k - 1, rows, :]
                pivot = 1.0 + lower_coef + upper_coef - upper_coef * ratio
                carried = (source + upper_coef * carried) / pivot
            ratio = lower_coef / pivot
            ratio_ref[layer_k, rows, :] = ratio
            wet_ref[layer_k, rows, :] = carried
        solved = carried
        drain_ref[...] = diff_ref[depth - 1, rows, :] * carried
        for layer_k in range(depth - 2, -1, -1):
            solved = wet_ref[layer_k, rows, :] + ratio_ref[layer_k, rows, :] * solved
            wet_ref[layer_k, rows, :] = solved
        return carry

    body(0, 0)


def column_solve(moisture, diffusivity, rain):
    blocks, depth, lanes = moisture.shape
    layered = (depth, blocks, lanes)
    return pl.pallas_call(
        column_kernel,
        out_shape=(
            jax.ShapeDtypeStruct(layered, jnp.float32),
            jax.ShapeDtypeStruct((blocks, lanes), jnp.float32),
        ),
        in_specs=[pl.BlockSpec(memory_space=pltpu.VMEM)] * 3,
        out_specs=(pl.BlockSpec(memory_space=pltpu.VMEM), pl.BlockSpec(memory_space=pltpu.VMEM)),
        scratch_shapes=[pltpu.VMEM(layered, jnp.float32)],
        cost_estimate=pl.CostEstimate(
            flops=12 * blocks * depth * lanes, transcendentals=0, bytes_accessed=12 * blocks * depth * lanes
        ),
    )(jnp.transpose(moisture, (1, 0, 2)), jnp.transpose(diffusivity, (1, 0, 2)), rain)


SHIFTS = ((0, 1), (2, 1), (1, 0), (1, 2))


def conductances(padded_cond):
    inner_rows = padded_cond.shape[1] - 2
    inner_cols = padded_cond.shape[2] - 2
    centre_cond = padded_cond[:, 1:-1, 1:-1]
    sides = []
    for row_shift, col_shift in SHIFTS:
        beside_cond = padded_cond[
            :, row_shift : row_shift + inner_rows, col_shift : col_shift + inner_cols
        ]
        sides.append(0.5 * (centre_cond + beside_cond))
    sides.append(0.5 * (centre_cond[1:] + centre_cond[:-1]))
    return sides


def lateral_core(padded_head, sides):
    inner_rows = padded_head.shape[1] - 2
    inner_cols = padded_head.shape[2] - 2
    centre = padded_head[:, 1:-1, 1:-1]
    flux_total = jnp.zeros_like(centre)
    for (row_shift, col_shift), side in zip(SHIFTS, sides):
        beside = padded_head[
            :, row_shift : row_shift + inner_rows, col_shift : col_shift + inner_cols
        ]
        flux_total = flux_total + side * (beside - centre)
    vertical = sides[4] * (centre[1:] - centre[:-1])
    flux_total = (
        flux_total
        + jnp.pad(vertical, ((0, 1), (0, 0), (0, 0)))
        - jnp.pad(vertical, ((1, 0), (0, 0), (0, 0)))
    )
    return centre + flow_rate * flux_total


def local(moisture, diffusivity, rain, head, conductivity, tile_ids, offsets, patch_ids, counts):
    highest = lax.Precision.HIGHEST
    block_count = moisture.shape[0]
    tile_count = lax.axis_size("gy")
    capacity = block_count // 2
    tile_rows = head.shape[1]
    tile_cols = head.shape[2]
    wet, drain = column_solve(moisture, diffusivity, rain)
    depth = moisture.shape[1]
    bottom = wet[depth - 1]
    in_use = jnp.arange(block_count, dtype=jnp.int32) < counts[0]
    in_use_f = in_use.astype(jnp.float32)
    to_tile = (
        (tile_ids[:, None] == jnp.arange(tile_count, dtype=jnp.int32)[None, :]) & in_use[:, None]
    ).astype(jnp.int32)
    earlier = (
        jnp.arange(block_count, dtype=jnp.int32)[None, :]
        < jnp.arange(block_count, dtype=jnp.int32)[:, None]
    ).astype(jnp.float32)
    before = jnp.dot(earlier, to_tile.astype(jnp.float32), precision=highest).astype(jnp.int32)
    slot_of = jnp.sum(before * to_tile, axis=1)
    slot_match = slot_of[None, None, :] == jnp.arange(capacity, dtype=jnp.int32)[None, :, None]
    placing = (to_tile.T[:, None, :] * slot_match).astype(jnp.float32)
    outgoing = jnp.einsum("tcb,bj->tcj", placing, drain, precision=highest)
    out_rows = (
        jnp.einsum("tcb,b->tc", placing, (offsets + 1).astype(jnp.float32), precision=highest) - 1.0
    )
    packed = jnp.concatenate(
        [outgoing, jnp.pad(out_rows, ((0, 0), (0, tile_cols - capacity)))[:, None, :]], axis=1
    )
    arrived = lax.all_to_all(packed, "gy", split_axis=0, concat_axis=0, tiled=True)
    incoming = arrived[:, :capacity, :]
    in_rows = arrived[:, capacity, :capacity]
    slot_total = tile_count * capacity
    landing = (
        in_rows.reshape(1, slot_total) == jnp.arange(tile_rows, dtype=jnp.float32)[:, None]
    ).astype(jnp.float32)
    recharge = jnp.dot(landing, incoming.reshape(slot_total, tile_cols), precision=highest)
    field = head.at[0].add(recharge)
    layers = field.shape[0]
    stacked = jnp.concatenate([field, conductivity], axis=0)
    rows_count = lax.axis_size("gx")
    rows_end = rows_count - 1
    dense = (stacked.shape[0] * SWEEPS, tile_cols)
    from_above = lax.ppermute(
        stacked[:, tile_rows - SWEEPS :, :].reshape(dense),
        "gx",
        [(i, i + 1) for i in range(rows_end)],
    )
    from_below = lax.ppermute(
        stacked[:, :SWEEPS, :].reshape(dense), "gx", [(i + 1, i) for i in range(rows_end)]
    )
    halo_shape = (stacked.shape[0], SWEEPS, tile_cols)
    rowed = jnp.concatenate(
        [from_above.reshape(halo_shape), stacked, from_below.reshape(halo_shape)], axis=1
    )
    halo_rows = rowed.shape[1]
    tiled_rows = -(-halo_rows // 8) * 8
    flat = jnp.pad(rowed, ((0, 0), (0, tiled_rows - halo_rows), (0, 0))).reshape(-1, tile_cols)
    picks = jnp.arange(SWEEPS, dtype=jnp.int32)[:, None]
    lanes = jnp.arange(tile_cols, dtype=jnp.int32)[None, :]
    by_lane = (((1,), (1,)), ((), ()))
    spare = jnp.zeros((8 - SWEEPS % 8) % 8, jnp.int32)[:, None] - 1
    choose = jnp.concatenate(
        [lanes == jnp.concatenate([picks, spare]), lanes == tile_cols - SWEEPS + picks], axis=0
    ).astype(jnp.float32)
    strips = lax.dot_general(choose, flat, by_lane, precision=highest)
    gap = SWEEPS + spare.shape[0]
    left_strip = strips[:SWEEPS]
    right_strip = strips[gap : gap + SWEEPS]
    ends = tile_count - 1
    strip_shape = left_strip.shape
    packed_strip = (strip_shape[0] * strip_shape[1] // tile_cols, tile_cols)
    from_left = lax.ppermute(
        right_strip.reshape(packed_strip), "gy", [(i, i + 1) for i in range(ends)]
    ).reshape(strip_shape)
    from_right = lax.ppermute(
        left_strip.reshape(packed_strip), "gy", [(i + 1, i) for i in range(ends)]
    ).reshape(strip_shape)
    width = tile_cols + 2 * SWEEPS
    out_lanes = jnp.arange(width, dtype=jnp.int32)[None, :]
    side = jnp.dot(
        jnp.concatenate([from_left, from_right], axis=0).T,
        jnp.concatenate(
            [out_lanes == picks, out_lanes == tile_cols + SWEEPS + picks], axis=0
        ).astype(jnp.float32),
        precision=highest,
    )
    side = with_layout_constraint(side, Layout((0, 1)))
    middle = jnp.pad(flat, ((0, 0), (SWEEPS, SWEEPS)))
    both = (middle + side).reshape(stacked.shape[0], tiled_rows, width)[:, :halo_rows, :]
    field = both[:layers]
    padded_cond = both[layers:]
    row_at = (
        lax.axis_index("gx") * tile_rows - SWEEPS + jnp.arange(tile_rows + 2 * SWEEPS)
    )[:, None]
    col_at = (
        lax.axis_index("gy") * tile_cols - SWEEPS + jnp.arange(tile_cols + 2 * SWEEPS)
    )[None, :]
    inside = (
        (row_at >= 0)
        & (row_at < tile_rows * lax.axis_size("gx"))
        & (col_at >= 0)
        & (col_at < tile_cols * tile_count)
    )
    sides = conductances(padded_cond)
    for sweep_k in range(SWEEPS):
        window = [
            side[:, sweep_k : side.shape[1] - sweep_k, sweep_k : side.shape[2] - sweep_k]
            for side in sides
        ]
        field = lateral_core(field, window)
        if sweep_k < SWEEPS - 1:
            edge = sweep_k + 1
            field = jnp.where(inside[None, edge:-edge, edge:-edge], field, 0.0)
    surface = field[0]
    answered = jnp.dot(landing.T, surface, precision=highest).reshape(
        tile_count, capacity, tile_cols
    )
    returned = lax.all_to_all(answered, "gy", split_axis=0, concat_axis=0, tiled=True)
    saturation = jnp.einsum("tcb,tcj->bj", placing, returned, precision=highest)
    new_bottom = bottom + capillary * (saturation - in_use_f[:, None] * bottom)
    moisture_out = jnp.transpose(wet.at[depth - 1].set(new_bottom), (1, 0, 2))
    patch_hot = (patch_ids[None, :] == jnp.arange(PATCH_DEV, dtype=jnp.int32)[:, None]).astype(
        jnp.float32
    )
    patch_sums = jnp.dot(patch_hot, saturation, precision=highest)
    return (field, moisture_out, patch_sums)


def solution(mesh):
    placed = (
        P(("gx", "gy"), None, None),
        P(("gx", "gy"), None, None),
        P(("gx", "gy"), None),
        P(None, "gx", "gy"),
        P(None, "gx", "gy"),
        P(("gx", "gy")),
        P(("gx", "gy")),
        P(("gx", "gy")),
        P(("gx", "gy")),
    )
    return jax.shard_map(
        local,
        mesh=mesh,
        in_specs=placed,
        out_specs=(P(None, "gx", "gy"), P(("gx", "gy"), None, None), P(("gx", "gy"), None)),
        check_vma=False,
    )
```
